768 devices in a mesh: ctx: 384 (over z_lo, y, x, core), head: 2 (over z_hi).
Axes of the slice: x: 4, y: 8, z: 12 (z_hi: 2, z_lo: 6; z = z_hi * 6 + z_lo), core: 2. Of those that a mesh axis runs over, the one named last changes fastest.
Arguments:
- document_lengths: int32 [192], replicated, may hold values from 1 to 512, 49152 in all
- delta_query: bfloat16 [49152, 8, 128], P('ctx', 'head'), may hold values from -6 to 6
- delta_keys: bfloat16 [49152, 8, 128], P('ctx', 'head'), may hold values from -6 to 6
- delta_values: bfloat16 [49152, 16, 128], P('ctx', 'head'), may hold values from -6 to 6
- write_strength: float32 [49152, 16], P('ctx', 'head'), may hold values from 0.2 to 0.5
- log_decay: float32 [49152, 16], P('ctx', 'head'), may hold values from -0.7 to 0
- saved_state: float32 [384, 16, 128, 128], P('ctx', 'head'), may hold values from -3 to 3
- delta_cotangent: bfloat16 [49152, 16, 128], P('ctx', 'head'), may hold values from -6 to 6
- soft_query: bfloat16 [49152, 8, 256], P('ctx', 'head'), may hold values from -5 to 5
- soft_keys: bfloat16 [49152, 2, 256], P('ctx', 'head'), may hold values from -5 to 5
- soft_values: bfloat16 [49152, 2, 256], P('ctx', 'head'), may hold values from -6 to 6
- gate_logits: bfloat16 [49152, 8, 256], P('ctx', 'head'), may hold values from -8 to 8
- soft_cotangent: bfloat16 [49152, 8, 256], P('ctx', 'head'), may hold values from -6 to 6
- gate_weight: bfloat16 [2048, 8, 256], P(None, 'head'), may hold values from -0.125 to 0.125
Outputs:
- readout_grad: float32 [49152, 8, 128], P('ctx', 'head')
- address_grad: float32 [49152, 8, 128], P('ctx', 'head')
- content_grad: float32 [49152, 16, 128], P('ctx', 'head')
- strength_grad: float32 [49152, 16], P('ctx', 'head')
- decay_grad: float32 [49152, 16], P('ctx', 'head')
- query_grad: float32 [49152, 8, 256], P('ctx', 'head')
- keys_grad: float32 [49152, 2, 256], P('ctx', 'head')
- values_grad: float32 [49152, 2, 256], P('ctx', 'head')
- input_grad: float32 [49152, 2048], P(('ctx', 'head'))
The draws below stay inside these ranges and needn't reach their ends.
Inputs may be any that keep to these rules, and one draw needn't show every extreme that they name: `document_lengths`: the lengths in tokens of 192 documents packed in order along the sequence; they sum to 49152, and the longest has exactly 512 tokens.
All inputs are finite; a program needn't handle non-finite values.
Results may differ from the reference program's by a relative error of at most 0.03.
Values may be sent and summed in bfloat16 or wider, within the bound.
No kernel may reach another device: no remote copies, remote signals or barrier semaphores. Data moves between devices by JAX's collectives and lax.ppermute only.
A program may use at most 64 MiB of HBM per device.

```python
import math
from functools import partial
import jax
import jax.numpy as jnp
import numpy as np
from jax import lax

D = 2048
QH = 8
KVH = 2
HD = 256
KH = 8
VALUE_HEADS = 16
DK = 128
BLOCK_TOKENS = 128
HOPS = 4
BLOCKS = 384
SEQUENCE_TOKENS = 49152
DOC_MOST = 512
NDOCS = 192


def draw_delta_keys(key, part):
    block_key, head_key, noise_key = jax.random.split(jax.random.fold_in(key, 17), 3)
    block_common = jax.random.normal(block_key, (BLOCKS, 1, KH, DK))
    head_common = jax.random.normal(head_key, (1, 1, KH, DK))
    noise = jax.random.normal(noise_key, (BLOCKS, BLOCK_TOKENS, KH, DK))
    values = 1.2 * block_common + 0.8 * head_common + noise
    values = jnp.clip(values, -6.0, 6.0)
    return values.reshape(SEQUENCE_TOKENS, KH, DK).astype(jnp.bfloat16)


def draw_log_decay(key, part):
    selection_key, gradual_decay_key, quick_decay_key, block_random_key, coarse_random_key, spike_random_key, layer_depth_key = jax.random.split(jax.random.fold_in(key, 3), 7)
    slow_share = 0.5
    slow_head = jax.random.uniform(selection_key, (VALUE_HEADS,)) < slow_share
    slow_rate = jnp.exp(jax.random.uniform(gradual_decay_key, (VALUE_HEADS,), minval=jnp.log(0.1), maxval=jnp.log(0.7))) / DOC_MOST
    fast_rate = jnp.exp(jax.random.uniform(quick_decay_key, (VALUE_HEADS,), minval=jnp.log(1.0 / 50.0), maxval=jnp.log(1.0 / 30.0)))
    base_rate = jnp.where(slow_head, slow_rate, fast_rate)
    block_factor = jnp.exp(jax.random.uniform(block_random_key, (BLOCKS, 1, VALUE_HEADS), minval=jnp.log(0.5), maxval=jnp.log(2.0)))
    rough = jax.random.uniform(coarse_random_key, (BLOCKS, BLOCK_TOKENS, VALUE_HEADS), minval=0.5, maxval=1.5)
    decay_speed = (base_rate[None, None, :] * block_factor * rough).reshape(SEQUENCE_TOKENS, VALUE_HEADS)
    spike_factor = jax.random.uniform(spike_random_key, (SEQUENCE_TOKENS, VALUE_HEADS)) < 1.0 / (2.0 * BLOCK_TOKENS)
    layer_depth = jnp.log(jax.random.uniform(layer_depth_key, (SEQUENCE_TOKENS, VALUE_HEADS), minval=0.5, maxval=0.8))
    return jnp.where(spike_factor, layer_depth, -decay_speed).astype(jnp.float32)


def draw_soft_query(key, part):
    base_key = jax.random.fold_in(key, 11)
    values = jnp.clip(jax.random.normal(base_key, (BLOCKS, BLOCK_TOKENS, QH, HD)), -5.0, 5.0)
    return values.reshape(SEQUENCE_TOKENS, QH, HD).astype(jnp.bfloat16)


def draw_soft_keys(key, part):
    base_key = jax.random.fold_in(key, 13)
    values = jnp.clip(jax.random.normal(base_key, (BLOCKS, BLOCK_TOKENS, KVH, HD)), -5.0, 5.0)
    return values.reshape(SEQUENCE_TOKENS, KVH, HD).astype(jnp.bfloat16)


def levels(key, shape, cuts, least, top_value):
    def one(dim, shards_of):
        heights = jax.random.uniform(jax.random.fold_in(jax.random.fold_in(key, 6), dim), (shards_of,), jnp.float32, least / len(cuts), top_value / len(cuts))
        return jnp.repeat(jnp.exp(heights), shape[dim] // shards_of).reshape((-1,) + (1,) * (len(shape) - dim - 1))

    gain = one(*cuts[0])
    for cut in cuts[1:]:
        gain = gain * one(*cut)
    return gain


def length_profile(number_of, total, reach, skew):
    loads = [(1 << 20) // math.isqrt(grade ** skew) + 1 for grade in range(2, number_of + 1)]
    surplus, given = total - reach - (number_of - 1), [1] * (number_of - 1)
    while surplus > 0:
        free = [i for i in range(number_of - 1) if given[i] < reach]
        pool, remaining = sum([loads[i] for i in free]), surplus
        for i in free:
            more = min(reach - given[i], max(1, remaining * loads[i] // pool), surplus)
            given[i] = given[i] + more
            surplus = surplus - more
    return np.array([reach] + given)


def uneven(key, number_of, total, reach, skew):
    if number_of == 2:
        one = jax.random.randint(key, (), max(1, total - reach), min(reach, total - 1) + 1)
        return jnp.stack([one, total - one])
    lengths = jnp.asarray(length_profile(number_of, total, reach, skew), jnp.int32)
    pairs = (number_of - 1) // 2
    source_of, receiver = lengths[1:1 + 2 * pairs:2], lengths[2:2 + 2 * pairs:2]
    margin = jnp.minimum(source_of - 1, reach - receiver)
    passed = jax.random.randint(jax.random.fold_in(key, 1), (pairs,), 0, 1 << 20) % (margin + 1)
    lengths = lengths.at[1:1 + 2 * pairs:2].set(source_of - passed).at[2:2 + 2 * pairs:2].set(receiver + passed)
    return lengths[jax.random.permutation(jax.random.fold_in(key, 2), number_of)]


def bell_draw(stream_key, shape, scale, most, shards=(), kind=jnp.bfloat16):
    drawn = jax.random.normal(stream_key, shape, jnp.float32) * scale
    if len(shards) > 0:
        drawn = levels(stream_key, shape, shards, -0.22, 0.18) * drawn
    return jnp.clip(drawn, min=-most, max=most).astype(kind)


def setup_inputs(seed: int = 0) -> dict:
    key_of = jax.random.split(jax.random.key(seed), 15)
    document_lengths = uneven(key_of[0], NDOCS, SEQUENCE_TOKENS, DOC_MOST, 1).astype(jnp.int32)
    delta_query = bell_draw(key_of[1], (SEQUENCE_TOKENS, KH, DK), 1.0, 6.0, ((0, 384), (1, 2)))
    delta_keys = draw_delta_keys(jax.random.fold_in(key_of[14], 71), 0)
    delta_values = bell_draw(key_of[3], (SEQUENCE_TOKENS, VALUE_HEADS, DK), 1.0, 6.0, ((0, 384), (1, 2)))
    write_strength = jnp.clip(jnp.exp(math.log(0.5) - 0.9162907 * jax.random.uniform(key_of[4], (SEQUENCE_TOKENS, VALUE_HEADS), jnp.float32) ** levels(key_of[4], (SEQUENCE_TOKENS, VALUE_HEADS), ((0, 384), (1, 2)), -0.2, 0.2)), 0.2, 0.5)
    log_decay = draw_log_decay(jax.random.fold_in(key_of[14], 71), 0)
    saved_state = bell_draw(key_of[6], (BLOCKS, VALUE_HEADS, DK, DK), 0.5, 3.0, ((0, 384), (1, 2)), jnp.float32)
    delta_cotangent = bell_draw(key_of[7], (SEQUENCE_TOKENS, VALUE_HEADS, DK), 1.0, 6.0, ((0, 384), (1, 2)))
    soft_query = draw_soft_query(jax.random.fold_in(key_of[14], 71), 0)
    soft_keys = draw_soft_keys(jax.random.fold_in(key_of[14], 71), 0)
    soft_values = bell_draw(key_of[10], (SEQUENCE_TOKENS, KVH, HD), 1.0, 6.0, ((0, 384), (1, 2)))
    gate_logits = bell_draw(key_of[11], (SEQUENCE_TOKENS, QH, HD), 2.0, 8.0, ((0, 384), (1, 2)))
    soft_cotangent = bell_draw(key_of[12], (SEQUENCE_TOKENS, QH, HD), 1.0, 6.0, ((0, 384), (1, 2)))
    gate_weight = bell_draw(key_of[13], (D, QH, HD), D ** -0.5, 0.125, ((1, 2),))
    return {"document_lengths": document_lengths, "delta_query": delta_query, "delta_keys": delta_keys, "delta_values": delta_values, "write_strength": write_strength, "log_decay": log_decay, "saved_state": saved_state, "delta_cotangent": delta_cotangent, "soft_query": soft_query, "soft_keys": soft_keys, "soft_values": soft_values, "gate_logits": gate_logits, "soft_cotangent": soft_cotangent, "gate_weight": gate_weight}


def segment_of(positions, doc_starts):
    return lax.optimization_barrier(jnp.sum((doc_starts[None, :] <= positions[:, None]).astype(jnp.int32), axis=1)) - 1

def delta_block(queries, key_rows, value_rows, strength, decay_rows, start_state, segment, continued):
    head_size = queries.shape[-1]
    repeat = value_rows.shape[1] // queries.shape[1]
    highest = lax.Precision.HIGHEST
    unit_query = queries * lax.rsqrt(lax.optimization_barrier(jnp.sum(queries * queries, axis=-1, keepdims=True)) + 1e-06) * head_size ** (-0.5)
    unit_key = key_rows * lax.rsqrt(lax.optimization_barrier(jnp.sum(key_rows * key_rows, axis=-1, keepdims=True)) + 1e-06)
    unit_query = jnp.repeat(unit_query, repeat, axis=1)
    unit_key = jnp.repeat(unit_key, repeat, axis=1)
    length = segment.shape[0]
    offsets = jnp.arange(length)
    cumulative = jnp.cumsum(decay_rows, axis=0).T
    same_doc = segment[:, None] == segment[None, :]
    causal = offsets[:, None] >= offsets[None, :]
    strictly = offsets[:, None] > offsets[None, :]
    spread = cumulative[:, :, None] - cumulative[:, None, :]
    inclusive = jnp.exp(jnp.where(same_doc & causal, spread, -jnp.inf))
    exclusive = jnp.where(strictly, inclusive, 0.0)
    carried = jnp.exp(cumulative) * continued.astype(jnp.float32)[None, :]
    key_key = jnp.einsum('thd,shd->hts', unit_key, unit_key, precision=highest)
    query_key = jnp.einsum('thd,shd->hts', unit_query, unit_key, precision=highest)
    strength_heads = strength.T
    system = jnp.eye(length, dtype=jnp.float32) + strength_heads[:, :, None] * key_key * exclusive
    recalled = jnp.einsum('thk,hvk->htv', unit_key, start_state, precision=highest)
    target = strength_heads[:, :, None] * (value_rows.transpose(1, 0, 2) - carried[:, :, None] * recalled)
    solver = partial(jax.scipy.linalg.solve_triangular, lower=True, unit_diagonal=True)
    written = jax.vmap(solver)(system, target)
    readout = carried[:, :, None] * jnp.einsum('thk,hvk->htv', unit_query, start_state, precision=highest)
    readout = readout + jnp.einsum('hts,hsv->htv', query_key * inclusive, written, precision=highest)
    last_doc = segment == segment[-1]
    fading = jnp.exp(jnp.where(last_doc[None, :], cumulative[:, -1:] - cumulative, -jnp.inf))
    final_state = carried[:, -1][:, None, None] * start_state
    final_state = final_state + jnp.einsum('htv,thk->hvk', written * fading[:, :, None], unit_key, precision=highest)
    return (readout.transpose(1, 0, 2), final_state)

def reference(document_lengths, delta_query, delta_keys, delta_values, write_strength, log_decay, saved_state, delta_cotangent, soft_query, soft_keys, soft_values, gate_logits, soft_cotangent, gate_weight):
    doc_starts = (jnp.cumsum(document_lengths) - document_lengths).astype(jnp.int32)
    positions = jnp.arange(SEQUENCE_TOKENS, dtype=jnp.int32)
    segment = segment_of(positions, doc_starts)
    continued = segment == segment_of(positions // BLOCK_TOKENS * BLOCK_TOKENS - 1, doc_starts)

    def blocked(array):
        return array.reshape((BLOCKS, BLOCK_TOKENS) + array.shape[1:])
    inputs = (blocked(delta_query.astype(jnp.float32)), blocked(delta_keys.astype(jnp.float32)), blocked(delta_values.astype(jnp.float32)), blocked(write_strength), blocked(log_decay), saved_state, blocked(segment), blocked(continued), blocked(delta_cotangent.astype(jnp.float32)))

    def backward_step(carry_grad, block_inputs):
        queries, key_rows, value_rows, strength, decay_rows, start_state, segment_row, continued_row, cotangent = block_inputs

        def forward(queries_in, keys_in, values_in, strength_in, decay_in, state_in):
            return delta_block(queries_in, keys_in, values_in, strength_in, decay_in, state_in, segment_row, continued_row)
        unused, pullback = jax.vjp(forward, queries, key_rows, value_rows, strength, decay_rows, start_state)
        gradients = pullback((cotangent, carry_grad))
        return (gradients[5], gradients[:5])
    ignored, delta_grads = lax.scan(backward_step, jnp.zeros((VALUE_HEADS, DK, DK), jnp.float32), inputs, reverse=True)
    readout_grad, address_grad, content_grad, strength_grad, decay_grad = [piece.reshape((SEQUENCE_TOKENS,) + piece.shape[2:]) for piece in delta_grads]
    group = QH // KVH
    score_scale = HD ** (-0.5)
    window = (HOPS + 1) * BLOCK_TOKENS
    queries_all = soft_query.astype(jnp.float32).reshape(SEQUENCE_TOKENS, KVH, group, HD)
    keys_all = soft_keys.astype(jnp.float32)
    values_all = soft_values.astype(jnp.float32)
    gate_open = jax.nn.sigmoid(gate_logits.astype(jnp.float32)).reshape(SEQUENCE_TOKENS, KVH, group, HD)
    upstream = soft_cotangent.astype(jnp.float32).reshape(SEQUENCE_TOKENS, KVH, group, HD)
    back = lax.optimization_barrier((upstream * gate_open).astype(jnp.bfloat16)).astype(jnp.float32)
    padding = jnp.zeros((HOPS * BLOCK_TOKENS, KVH, HD), jnp.float32)
    keys_front = jnp.concatenate([padding, keys_all], axis=0)
    values_front = jnp.concatenate([padding, values_all], axis=0)

    def query_block(index):
        first = index * BLOCK_TOKENS
        block_query = lax.dynamic_slice_in_dim(queries_all, first, BLOCK_TOKENS, 0)
        block_back = lax.dynamic_slice_in_dim(back, first, BLOCK_TOKENS, 0)
        window_keys = lax.dynamic_slice_in_dim(keys_front, first, window, 0)
        window_values = lax.dynamic_slice_in_dim(values_front, first, window, 0)
        query_positions = first + jnp.arange(BLOCK_TOKENS, dtype=jnp.int32)
        key_positions = first - HOPS * BLOCK_TOKENS + jnp.arange(window, dtype=jnp.int32)
        keep = segment_of(query_positions, doc_starts)[:, None] == segment_of(key_positions, doc_starts)[None, :]
        keep = keep & (key_positions[None, :] <= query_positions[:, None])
        scores = jnp.einsum('qkgd,tkd->kgqt', block_query, window_keys) * score_scale
        scores = jnp.where(keep, scores, -jnp.inf)
        peak = lax.optimization_barrier(jnp.max(scores, axis=-1, keepdims=True))
        log_total = peak + jnp.log(lax.optimization_barrier(jnp.sum(jnp.exp(scores - peak), axis=-1, keepdims=True)))
        weights = jnp.exp(scores - log_total)
        rounded = lax.optimization_barrier(weights.astype(jnp.bfloat16)).astype(jnp.float32)
        output = jnp.einsum('kgqt,tkd->qkgd', rounded, window_values)
        row_dot = lax.optimization_barrier(jnp.sum(block_back * output, axis=-1)).transpose(1, 2, 0)
        dprob = jnp.einsum('qkgd,tkd->kgqt', block_back, window_values)
        dscore = lax.optimization_barrier((weights * (dprob - row_dot[..., None])).astype(jnp.bfloat16)).astype(jnp.float32)
        block_grad = jnp.einsum('kgqt,tkd->qkgd', dscore, window_keys) * score_scale
        return (output, log_total[..., 0], row_dot, block_grad)
    outputs, log_totals, row_dots, query_grads = lax.map(query_block, jnp.arange(BLOCKS, dtype=jnp.int32))
    output_all = outputs.reshape(SEQUENCE_TOKENS, KVH, group, HD)
    query_grad = query_grads.reshape(SEQUENCE_TOKENS, QH, HD)
    total_tokens = log_totals.transpose(0, 3, 1, 2).reshape(SEQUENCE_TOKENS, KVH, group)
    dot_tokens = row_dots.transpose(0, 3, 1, 2).reshape(SEQUENCE_TOKENS, KVH, group)
    tail = HOPS * BLOCK_TOKENS
    queries_tail = jnp.concatenate([queries_all, jnp.zeros((tail, KVH, group, HD), jnp.float32)], axis=0)
    back_tail = jnp.concatenate([back, jnp.zeros((tail, KVH, group, HD), jnp.float32)], axis=0)
    total_tail = jnp.concatenate([total_tokens, jnp.zeros((tail, KVH, group), jnp.float32)], axis=0)
    dot_tail = jnp.concatenate([dot_tokens, jnp.zeros((tail, KVH, group), jnp.float32)], axis=0)

    def key_block(index):
        first = index * BLOCK_TOKENS
        block_keys = lax.dynamic_slice_in_dim(keys_all, first, BLOCK_TOKENS, 0)
        block_values = lax.dynamic_slice_in_dim(values_all, first, BLOCK_TOKENS, 0)
        window_query = lax.dynamic_slice_in_dim(queries_tail, first, window, 0)
        window_back = lax.dynamic_slice_in_dim(back_tail, first, window, 0)
        window_total = lax.dynamic_slice_in_dim(total_tail, first, window, 0)
        window_dot = lax.dynamic_slice_in_dim(dot_tail, first, window, 0)
        query_positions = first + jnp.arange(window, dtype=jnp.int32)
        key_positions = first + jnp.arange(BLOCK_TOKENS, dtype=jnp.int32)
        keep = segment_of(query_positions, doc_starts)[:, None] == segment_of(key_positions, doc_starts)[None, :]
        keep = keep & (key_positions[None, :] <= query_positions[:, None]) & (query_positions < SEQUENCE_TOKENS)[:, None]
        scores = jnp.einsum('qkgd,tkd->kgqt', window_query, block_keys) * score_scale
        weights = jnp.exp(jnp.where(keep, scores - window_total.transpose(1, 2, 0)[..., None], -jnp.inf))
        rounded = lax.optimization_barrier(weights.astype(jnp.bfloat16)).astype(jnp.float32)
        dprob = jnp.einsum('qkgd,tkd->kgqt', window_back, block_values)
        dscore = lax.optimization_barrier((weights * (dprob - window_dot.transpose(1, 2, 0)[..., None])).astype(jnp.bfloat16)).astype(jnp.float32)
        key_grad = jnp.einsum('kgqt,qkgd->tkd', dscore, window_query) * score_scale
        value_grad = jnp.einsum('kgqt,qkgd->tkd', rounded, window_back)
        return (key_grad, value_grad)
    key_grads, value_grads = lax.map(key_block, jnp.arange(BLOCKS, dtype=jnp.int32))
    keys_grad = key_grads.reshape(SEQUENCE_TOKENS, KVH, HD)
    values_grad = value_grads.reshape(SEQUENCE_TOKENS, KVH, HD)
    slope = (upstream * output_all * gate_open * (1.0 - gate_open)).astype(jnp.bfloat16).reshape(SEQUENCE_TOKENS, QH * HD)
    input_grad = jnp.dot(slope.astype(jnp.float32), gate_weight.reshape(D, QH * HD).T.astype(jnp.float32), preferred_element_type=jnp.float32)
    return (readout_grad, address_grad, content_grad, strength_grad, decay_grad, query_grad, keys_grad, values_grad, input_grad)
```

```python
import jax
import jax.numpy as jnp
from jax import lax
from jax.sharding import PartitionSpec as P

HOPS = 4


def shortened(x):
    return jax.tree.map(lambda a: a.astype(jnp.bfloat16) if a.dtype == jnp.float32 else a, x)


def from_behind(x, axis, by):
    peers = lax.axis_size(axis)
    pairs = [(i, i + by) for i in range(peers) if 0 <= i + by < peers]
    return lax.ppermute(x, axis, pairs)


def segment_of(positions, doc_starts):
    return jnp.sum((doc_starts[None, :] <= positions[:, None]).astype(jnp.int32), axis=1) - 1


def matmul(spec, a, b):
    return jnp.einsum(spec, a, b, precision=lax.Precision.HIGHEST)


def unit_lower_inverse(lower):
    n = lower.shape[-1]
    rows = jnp.arange(n)[:, None]
    cols = jnp.arange(n)[None, :]
    eye = jnp.eye(n, dtype=jnp.float32)
    first = (rows // 2 == cols // 2) & (rows % 2 == 1) & (cols % 2 == 0)
    inverse = eye - jnp.where(first, lower, 0.0)
    size = 2
    while size < n:
        mask = (rows // (2 * size) == cols // (2 * size)) & ((rows // size) % 2 == 1) & (
            (cols // size) % 2 == 0
        )
        block = jnp.where(mask, lower, 0.0)
        inverse = inverse - matmul("hij,hjk->hik", inverse, matmul("hij,hjk->hik", block, inverse))
        size *= 2
    return inverse


@jax.custom_vjp
def unit_lower_solve(lower, inverse, target):
    return matmul("hts,hsv->htv", inverse, target)


def unit_lower_solve_fwd(lower, inverse, target):
    written = matmul("hts,hsv->htv", inverse, target)
    return written, (inverse, written)


def unit_lower_solve_bwd(saved, grad):
    inverse, written = saved
    target_grad = matmul("hst,hsv->htv", inverse, grad)
    n = inverse.shape[-1]
    strict = jnp.arange(n)[:, None] > jnp.arange(n)[None, :]
    lower_grad = jnp.where(strict, -matmul("htv,hsv->hts", target_grad, written), 0.0)
    return lower_grad, jnp.zeros_like(inverse), target_grad


unit_lower_solve.defvjp(unit_lower_solve_fwd, unit_lower_solve_bwd)


def block_system(key_rows, strength, decay_rows, segment, repeat):
    unit_key = key_rows * lax.rsqrt(jnp.sum(key_rows * key_rows, axis=-1, keepdims=True) + 1e-06)
    unit_key = jnp.repeat(unit_key, repeat, axis=1)
    length = segment.shape[0]
    offsets = jnp.arange(length)
    cumulative = jnp.cumsum(decay_rows, axis=0).T
    same_doc = segment[:, None] == segment[None, :]
    causal = offsets[:, None] >= offsets[None, :]
    strictly = offsets[:, None] > offsets[None, :]
    spread = cumulative[:, :, None] - cumulative[:, None, :]
    inclusive = jnp.exp(jnp.where(same_doc & causal, spread, -jnp.inf))
    exclusive = jnp.where(strictly, inclusive, 0.0)
    key_key = jnp.einsum("thd,shd->hts", unit_key, unit_key, precision=lax.Precision.HIGHEST)
    return strength.T[:, :, None] * key_key * exclusive


def delta_block(
    queries, key_rows, value_rows, strength, decay_rows, start_state, segment, continued, inverse
):
    head_size = queries.shape[-1]
    repeat = value_rows.shape[1] // queries.shape[1]
    highest = lax.Precision.HIGHEST
    unit_query = (
        queries
        * lax.rsqrt(jnp.sum(queries * queries, axis=-1, keepdims=True) + 1e-06)
        * head_size ** (-0.5)
    )
    unit_key = key_rows * lax.rsqrt(jnp.sum(key_rows * key_rows, axis=-1, keepdims=True) + 1e-06)
    unit_query = jnp.repeat(unit_query, repeat, axis=1)
    unit_key = jnp.repeat(unit_key, repeat, axis=1)
    length = segment.shape[0]
    offsets = jnp.arange(length)
    cumulative = jnp.cumsum(decay_rows, axis=0).T
    same_doc = segment[:, None] == segment[None, :]
    causal = offsets[:, None] >= offsets[None, :]
    strictly = offsets[:, None] > offsets[None, :]
    spread = cumulative[:, :, None] - cumulative[:, None, :]
    inclusive = jnp.exp(jnp.where(same_doc & causal, spread, -jnp.inf))
    exclusive = jnp.where(strictly, inclusive, 0.0)
    carried = jnp.exp(cumulative) * continued.astype(jnp.float32)[None, :]
    key_key = jnp.einsum("thd,shd->hts", unit_key, unit_key, precision=highest)
    query_key = jnp.einsum("thd,shd->hts", unit_query, unit_key, precision=highest)
    strength_heads = strength.T
    system = jnp.eye(length, dtype=jnp.float32) + strength_heads[:, :, None] * key_key * exclusive
    recalled = jnp.einsum("thk,hvk->htv", unit_key, start_state, precision=highest)
    target = strength_heads[:, :, None] * (
        value_rows.transpose(1, 0, 2) - carried[:, :, None] * recalled
    )
    written = unit_lower_solve(system - jnp.eye(length, dtype=jnp.float32), inverse, target)
    readout = carried[:, :, None] * jnp.einsum(
        "thk,hvk->htv", unit_query, start_state, precision=highest
    )
    readout = readout + jnp.einsum(
        "hts,hsv->htv", query_key * inclusive, written, precision=highest
    )
    last_doc = segment == segment[-1]
    fading = jnp.exp(jnp.where(last_doc[None, :], cumulative[:, -1:] - cumulative, -jnp.inf))
    final_state = carried[:, -1][:, None, None] * start_state
    final_state = final_state + jnp.einsum(
        "htv,thk->hvk", written * fading[:, :, None], unit_key, precision=highest
    )
    return (readout.transpose(1, 0, 2), final_state)


def carry_back(incoming, mapping):
    return jnp.einsum("hvk,hjk->hvj", incoming, mapping, precision=lax.Precision.HIGHEST)


def shards(
    document_lengths,
    delta_query,
    delta_keys,
    delta_values,
    write_strength,
    log_decay,
    saved_state,
    delta_cotangent,
    soft_query,
    soft_keys,
    soft_values,
    gate_logits,
    soft_cotangent,
    gate_weight,
):
    length = delta_query.shape[0]
    block_index = lax.axis_index("ctx")
    offsets = jnp.arange(length, dtype=jnp.int32)
    doc_starts = jnp.cumsum(document_lengths) - document_lengths
    positions = block_index * length + offsets
    segment = segment_of(positions, doc_starts)
    before = segment_of(positions[:1] - 1, doc_starts)
    continued = segment == before[0]

    local_pair = jnp.stack([soft_keys, soft_values])
    arrived = [local_pair] + [from_behind(local_pair, "ctx", d) for d in range(1, HOPS + 1)]
    window_pair = jnp.concatenate(arrived[::-1], axis=1)

    queries = delta_query.astype(jnp.float32)
    key_rows = delta_keys.astype(jnp.float32)
    value_rows = delta_values.astype(jnp.float32)
    repeat = value_rows.shape[1] // queries.shape[1]
    inverse = lax.stop_gradient(
        unit_lower_inverse(block_system(key_rows, write_strength, log_decay, segment, repeat))
    )
    inverse, window_pair = lax.optimization_barrier((inverse, window_pair))

    kv_heads = soft_keys.shape[1]
    width = soft_keys.shape[2]
    group = soft_query.shape[1] // kv_heads
    score_scale = width ** (-0.5)
    key_positions = (block_index - HOPS) * length + jnp.arange((HOPS + 1) * length, dtype=jnp.int32)
    key_segment = segment_of(key_positions, doc_starts)
    keep = (segment[:, None] == key_segment[None, :]) & (
        key_positions[None, :] <= positions[:, None]
    )
    queries_four = soft_query.reshape(length, kv_heads, group, width)
    scores = (
        jnp.einsum(
            "qkgd,tkd->kgqt", queries_four, window_pair[0], preferred_element_type=jnp.float32
        )
        * score_scale
    )
    scores = jnp.where(keep, scores, -jnp.inf)
    peak = jnp.max(scores, axis=-1, keepdims=True)
    log_total = peak + jnp.log(jnp.sum(jnp.exp(scores - peak), axis=-1, keepdims=True))
    weights = jnp.exp(scores - log_total)
    rounded = weights.astype(jnp.bfloat16)
    output = jnp.einsum(
        "kgqt,tkd->qkgd", rounded, window_pair[1], preferred_element_type=jnp.float32
    )
    gate_open = jax.nn.sigmoid(gate_logits.astype(jnp.float32)).reshape(
        length, kv_heads, group, width
    )
    upstream = soft_cotangent.astype(jnp.float32).reshape(length, kv_heads, group, width)
    slope = (
        (upstream * output * gate_open * (1.0 - gate_open)).astype(jnp.bfloat16).reshape(length, -1)
    )
    weight_flat = gate_weight.reshape(gate_weight.shape[0], -1)
    gate_full = lax.dot_general(
        slope, weight_flat, (((1,), (1,)), ((), ())), preferred_element_type=jnp.float32
    )
    gate_part = gate_full.astype(jnp.bfloat16)
    gate_full, gate_part, inverse, queries, key_rows, value_rows = lax.optimization_barrier(
        (gate_full, gate_part, inverse, queries, key_rows, value_rows)
    )
    half = gate_part.shape[0] // 2
    head_index = lax.axis_index("head")
    kept = lax.dynamic_slice_in_dim(gate_full, head_index * half, half, 0)
    sent = lax.dynamic_slice_in_dim(gate_part, (1 - head_index) * half, half, 0)
    received = lax.ppermute(sent, "head", [(0, 1), (1, 0)])

    start_state = saved_state[0]
    cotangent = delta_cotangent.astype(jnp.float32)

    def forward_state(state_in):
        return delta_block(
            queries,
            key_rows,
            value_rows,
            write_strength,
            log_decay,
            state_in,
            segment,
            continued,
            inverse,
        )

    unused_state, state_pullback = jax.vjp(forward_state, start_state)
    own_part = state_pullback((cotangent, jnp.zeros_like(start_state)))[0]
    identity = jnp.broadcast_to(
        jnp.eye(start_state.shape[-1], dtype=jnp.float32), start_state.shape
    )
    transfer = delta_block(
        queries,
        key_rows,
        jnp.zeros_like(value_rows),
        write_strength,
        log_decay,
        identity,
        segment,
        continued,
        inverse,
    )[1]
    received, own_part, transfer = lax.optimization_barrier((received, own_part, transfer))
    input_grad = kept + received.astype(jnp.float32)
    gathered = own_part
    incoming = own_part
    for step_index in range(HOPS):
        incoming = from_behind(shortened(gathered), "ctx", -1).astype(gathered.dtype)
        gathered = own_part + carry_back(incoming, transfer)

    def forward(queries_in, keys_in, values_in, strength_in, decay_in):
        return delta_block(
            queries_in,
            keys_in,
            values_in,
            strength_in,
            decay_in,
            start_state,
            segment,
            continued,
            inverse,
        )

    unused, pullback = jax.vjp(forward, queries, key_rows, value_rows, write_strength, log_decay)
    readout_grad, address_grad, content_grad, strength_grad, decay_grad = pullback(
        (cotangent, incoming)
    )

    back = (upstream * gate_open).astype(jnp.bfloat16)
    row_dot = jnp.sum(back.astype(jnp.float32) * output, axis=-1).transpose(1, 2, 0)[..., None]
    dprob = jnp.einsum("qkgd,tkd->kgqt", back, window_pair[1], preferred_element_type=jnp.float32)
    dscore = (weights * (dprob - row_dot)).astype(jnp.bfloat16)
    query_grad = (
        jnp.einsum("kgqt,tkd->qkgd", dscore, window_pair[0], preferred_element_type=jnp.float32)
        * score_scale
    )
    query_grad = query_grad.reshape(length, kv_heads * group, width)
    key_part = (
        jnp.einsum("kgqt,qkgd->tkd", dscore, queries_four, preferred_element_type=jnp.float32)
        * score_scale
    )
    value_part = jnp.einsum("kgqt,qkgd->tkd", rounded, back, preferred_element_type=jnp.float32)
    returned = jnp.stack([key_part, value_part])

    def slab(distance):
        return returned[:, (HOPS - distance) * length : (HOPS - distance + 1) * length]

    summed = slab(0)
    for distance in range(1, HOPS + 1):
        summed = summed + from_behind(
            slab(distance).astype(jnp.bfloat16), "ctx", -distance
        ).astype(summed.dtype)
    return (
        readout_grad,
        address_grad,
        content_grad,
        strength_grad,
        decay_grad,
        query_grad,
        summed[0],
        summed[1],
        input_grad,
    )


def solution(mesh):
    placed = (
        P(),
        P("ctx", "head", None),
        P("ctx", "head", None),
        P("ctx", "head", None),
        P("ctx", "head"),
        P("ctx", "head"),
        P("ctx", "head", None, None),
        P("ctx", "head", None),
        P("ctx", "head", None),
        P("ctx", "head", None),
        P("ctx", "head", None),
        P("ctx", "head", None),
        P("ctx", "head", None),
        P(None, "head", None),
    )
    return jax.shard_map(
        shards,
        mesh=mesh,
        in_specs=placed,
        out_specs=(
            P("ctx", "head", None),
            P("ctx", "head", None),
            P("ctx", "head", None),
            P("ctx", "head"),
            P("ctx", "head"),
            P("ctx", "head", None),
            P("ctx", "head", None),
            P("ctx", "head", None),
            P(("ctx", "head"), None),
        ),
        check_vma=False,
    )
```

```python
import jax
import jax.numpy as jnp
from jax import lax
from jax.sharding import PartitionSpec as P

HOPS = 4


def shortened(x):
    return jax.tree.map(lambda a: a.astype(jnp.bfloat16) if a.dtype == jnp.float32 else a, x)


def from_behind(x, axis, by):
    peers = lax.axis_size(axis)
    pairs = [(i, i + by) for i in range(peers) if 0 <= i + by < peers]
    return lax.ppermute(x, axis, pairs)


def segment_of(positions, doc_starts):
    return jnp.sum((doc_starts[None, :] <= positions[:, None]).astype(jnp.int32), axis=1) - 1


def matmul(spec, a, b):
    return jnp.einsum(spec, a, b, precision=lax.Precision.HIGHEST)


def unit_lower_inverse(lower):
    n = lower.shape[-1]
    rows = jnp.arange(n)[:, None]
    cols = jnp.arange(n)[None, :]
    eye = jnp.eye(n, dtype=jnp.float32)
    first = (rows // 2 == cols // 2) & (rows % 2 == 1) & (cols % 2 == 0)
    inverse = eye - jnp.where(first, lower, 0.0)
    size = 2
    while size < n:
        mask = (rows // (2 * size) == cols // (2 * size)) & ((rows // size) % 2 == 1) & (
            (cols // size) % 2 == 0
        )
        block = jnp.where(mask, lower, 0.0)
        inverse = inverse - matmul("hij,hjk->hik", inverse, matmul("hij,hjk->hik", block, inverse))
        size *= 2
    return inverse


@jax.custom_vjp
def unit_lower_solve(lower, inverse, target):
    return matmul("hts,hsv->htv", inverse, target)


def unit_lower_solve_fwd(lower, inverse, target):
    written = matmul("hts,hsv->htv", inverse, target)
    return written, (inverse, written)


def unit_lower_solve_bwd(saved, grad):
    inverse, written = saved
    target_grad = matmul("hst,hsv->htv", inverse, grad)
    n = inverse.shape[-1]
    strict = jnp.arange(n)[:, None] > jnp.arange(n)[None, :]
    lower_grad = jnp.where(strict, -matmul("htv,hsv->hts", target_grad, written), 0.0)
    return lower_grad, jnp.zeros_like(inverse), target_grad


unit_lower_solve.defvjp(unit_lower_solve_fwd, unit_lower_solve_bwd)


def block_system(key_rows, strength, decay_rows, segment, repeat):
    unit_key = key_rows * lax.rsqrt(jnp.sum(key_rows * key_rows, axis=-1, keepdims=True) + 1e-06)
    unit_key = jnp.repeat(unit_key, repeat, axis=1)
    length = segment.shape[0]
    offsets = jnp.arange(length)
    cumulative = jnp.cumsum(decay_rows, axis=0).T
    same_doc = segment[:, None] == segment[None, :]
    causal = offsets[:, None] >= offsets[None, :]
    strictly = offsets[:, None] > offsets[None, :]
    spread = cumulative[:, :, None] - cumulative[:, None, :]
    inclusive = jnp.exp(jnp.where(same_doc & causal, spread, -jnp.inf))
    exclusive = jnp.where(strictly, inclusive, 0.0)
    key_key = jnp.einsum("thd,shd->hts", unit_key, unit_key, precision=lax.Precision.HIGHEST)
    return strength.T[:, :, None] * key_key * exclusive


def delta_block(
    queries, key_rows, value_rows, strength, decay_rows, start_state, segment, continued, inverse
):
    head_size = queries.shape[-1]
    repeat = value_rows.shape[1] // queries.shape[1]
    highest = lax.Precision.HIGHEST
    unit_query = (
        queries
        * lax.rsqrt(jnp.sum(queries * queries, axis=-1, keepdims=True) + 1e-06)
        * head_size ** (-0.5)
    )
    unit_key = key_rows * lax.rsqrt(jnp.sum(key_rows * key_rows, axis=-1, keepdims=True) + 1e-06)
    unit_query = jnp.repeat(unit_query, repeat, axis=1)
    unit_key = jnp.repeat(unit_key, repeat, axis=1)
    length = segment.shape[0]
    offsets = jnp.arange(length)
    cumulative = jnp.cumsum(decay_rows, axis=0).T
    same_doc = segment[:, None] == segment[None, :]
    causal = offsets[:, None] >= offsets[None, :]
    strictly = offsets[:, None] > offsets[None, :]
    spread = cumulative[:, :, None] - cumulative[:, None, :]
    inclusive = jnp.exp(jnp.where(same_doc & causal, spread, -jnp.inf))
    exclusive = jnp.where(strictly, inclusive, 0.0)
    carried = jnp.exp(cumulative) * continued.astype(jnp.float32)[None, :]
    key_key = jnp.einsum("thd,shd->hts", unit_key, unit_key, precision=highest)
    query_key = jnp.einsum("thd,shd->hts", unit_query, unit_key, precision=highest)
    strength_heads = strength.T
    system = jnp.eye(length, dtype=jnp.float32) + strength_heads[:, :, None] * key_key * exclusive
    recalled = jnp.einsum("thk,hvk->htv", unit_key, start_state, precision=highest)
    target = strength_heads[:, :, None] * (
        value_rows.transpose(1, 0, 2) - carried[:, :, None] * recalled
    )
    written = unit_lower_solve(system - jnp.eye(length, dtype=jnp.float32), inverse, target)
    readout = carried[:, :, None] * jnp.einsum(
        "thk,hvk->htv", unit_query, start_state, precision=highest
    )
    readout = readout + jnp.einsum(
        "hts,hsv->htv", query_key * inclusive, written, precision=highest
    )
    last_doc = segment == segment[-1]
    fading = jnp.exp(jnp.where(last_doc[None, :], cumulative[:, -1:] - cumulative, -jnp.inf))
    final_state = carried[:, -1][:, None, None] * start_state
    final_state = final_state + jnp.einsum(
        "htv,thk->hvk", written * fading[:, :, None], unit_key, precision=highest
    )
    return (readout.transpose(1, 0, 2), final_state)


def carry_back(incoming, mapping):
    return jnp.einsum("hvk,hjk->hvj", incoming, mapping, precision=lax.Precision.HIGHEST)


def shards(
    document_lengths,
    delta_query,
    delta_keys,
    delta_values,
    write_strength,
    log_decay,
    saved_state,
    delta_cotangent,
    soft_query,
    soft_keys,
    soft_values,
    gate_logits,
    soft_cotangent,
    gate_weight,
):
    length = delta_query.shape[0]
    block_index = lax.axis_index("ctx")
    offsets = jnp.arange(length, dtype=jnp.int32)
    doc_starts = jnp.cumsum(document_lengths) - document_lengths
    positions = block_index * length + offsets
    segment = segment_of(positions, doc_starts)
    before = segment_of(positions[:1] - 1, doc_starts)
    continued = segment == before[0]

    local_pair = jnp.stack([soft_keys, soft_values])
    arrived = [local_pair] + [from_behind(local_pair, "ctx", d) for d in range(1, HOPS + 1)]
    window_pair = jnp.concatenate(arrived[::-1], axis=1)

    queries = delta_query.astype(jnp.float32)
    key_rows = delta_keys.astype(jnp.float32)
    value_rows = delta_values.astype(jnp.float32)
    repeat = value_rows.shape[1] // queries.shape[1]
    inverse = lax.stop_gradient(
        unit_lower_inverse(block_system(key_rows, write_strength, log_decay, segment, repeat))
    )
    inverse, window_pair = lax.optimization_barrier((inverse, window_pair))

    kv_heads = soft_keys.shape[1]
    width = soft_keys.shape[2]
    group = soft_query.shape[1] // kv_heads
    score_scale = width ** (-0.5)
    key_positions = (block_index - HOPS) * length + jnp.arange((HOPS + 1) * length, dtype=jnp.int32)
    key_segment = segment_of(key_positions, doc_starts)
    keep = (segment[:, None] == key_segment[None, :]) & (
        key_positions[None, :] <= positions[:, None]
    )
    queries_four = soft_query.reshape(length, kv_heads, group, width)
    scores = (
        jnp.einsum(
            "qkgd,tkd->kgqt", queries_four, window_pair[0], preferred_element_type=jnp.float32
        )
        * score_scale
    )
    scores = jnp.where(keep, scores, -jnp.inf)
    peak = jnp.max(scores, axis=-1, keepdims=True)
    log_total = peak + jnp.log(jnp.sum(jnp.exp(scores - peak), axis=-1, keepdims=True))
    weights = jnp.exp(scores - log_total)
    rounded = weights.astype(jnp.bfloat16)
    output = jnp.einsum(
        "kgqt,tkd->qkgd", rounded, window_pair[1], preferred_element_type=jnp.float32
    )
    gate_open = jax.nn.sigmoid(gate_logits.astype(jnp.float32)).reshape(
        length, kv_heads, group, width
    )
    upstream = soft_cotangent.astype(jnp.float32).reshape(length, kv_heads, group, width)
    slope = (
        (upstream * output * gate_open * (1.0 - gate_open))
        .astype(jnp.bfloat16)
        .reshape(length, kv_heads * group, width)
    )
    gate_full = lax.dot_general(
        slope, gate_weight, (((1, 2), (1, 2)), ((), ())), preferred_element_type=jnp.float32
    )
    gate_part = gate_full.astype(jnp.bfloat16)
    gate_full, gate_part, inverse, queries, key_rows, value_rows = lax.optimization_barrier(
        (gate_full, gate_part, inverse, queries, key_rows, value_rows)
    )
    half = gate_part.shape[0] // 2
    head_index = lax.axis_index("head")
    kept = lax.dynamic_slice_in_dim(gate_full, head_index * half, half, 0)
    sent = lax.dynamic_slice_in_dim(gate_part, (1 - head_index) * half, half, 0)
    received = lax.ppermute(sent, "head", [(0, 1), (1, 0)])

    start_state = saved_state[0]
    cotangent = delta_cotangent.astype(jnp.float32)

    def forward_state(state_in):
        return delta_block(
            queries,
            key_rows,
            value_rows,
            write_strength,
            log_decay,
            state_in,
            segment,
            continued,
            inverse,
        )

    unused_state, state_pullback = jax.vjp(forward_state, start_state)
    own_part = state_pullback((cotangent, jnp.zeros_like(start_state)))[0]
    identity = jnp.broadcast_to(
        jnp.eye(start_state.shape[-1], dtype=jnp.float32), start_state.shape
    )
    transfer = delta_block(
        queries,
        key_rows,
        jnp.zeros_like(value_rows),
        write_strength,
        log_decay,
        identity,
        segment,
        continued,
        inverse,
    )[1]
    gathered = own_part
    incoming = own_part
    for step_index in range(HOPS):
        incoming = from_behind(shortened(gathered), "ctx", -1).astype(gathered.dtype)
        gathered = own_part + carry_back(incoming, transfer)

    received, incoming = lax.optimization_barrier((received, incoming))
    input_grad = kept + received.astype(jnp.float32)

    def forward(queries_in, keys_in, values_in, strength_in, decay_in):
        return delta_block(
            queries_in,
            keys_in,
            values_in,
            strength_in,
            decay_in,
            start_state,
            segment,
            continued,
            inverse,
        )

    unused, pullback = jax.vjp(forward, queries, key_rows, value_rows, write_strength, log_decay)
    readout_grad, address_grad, content_grad, strength_grad, decay_grad = pullback(
        (cotangent, incoming)
    )

    back = (upstream * gate_open).astype(jnp.bfloat16)
    row_dot = jnp.sum(back.astype(jnp.float32) * output, axis=-1).transpose(1, 2, 0)[..., None]
    dprob = jnp.einsum("qkgd,tkd->kgqt", back, window_pair[1], preferred_element_type=jnp.float32)
    dscore = (weights * (dprob - row_dot)).astype(jnp.bfloat16)
    query_grad = (
        jnp.einsum("kgqt,tkd->qkgd", dscore, window_pair[0], preferred_element_type=jnp.float32)
        * score_scale
    )
    query_grad = query_grad.reshape(length, kv_heads * group, width)
    key_part = (
        jnp.einsum("kgqt,qkgd->tkd", dscore, queries_four, preferred_element_type=jnp.float32)
        * score_scale
    )
    value_part = jnp.einsum("kgqt,qkgd->tkd", rounded, back, preferred_element_type=jnp.float32)
    returned = jnp.stack([key_part, value_part])

    def slab(distance):
        return returned[:, (HOPS - distance) * length : (HOPS - distance + 1) * length]

    summed = slab(0)
    for distance in range(1, HOPS + 1):
        summed = summed + from_behind(
            slab(distance).astype(jnp.bfloat16), "ctx", -distance
        ).astype(summed.dtype)
    return (
        readout_grad,
        address_grad,
        content_grad,
        strength_grad,
        decay_grad,
        query_grad,
        summed[0],
        summed[1],
        input_grad,
    )


def solution(mesh):
    placed = (
        P(),
        P("ctx", "head", None),
        P("ctx", "head", None),
        P("ctx", "head", None),
        P("ctx", "head"),
        P("ctx", "head"),
        P("ctx", "head", None, None),
        P("ctx", "head", None),
        P("ctx", "head", None),
        P("ctx", "head", None),
        P("ctx", "head", None),
        P("ctx", "head", None),
        P("ctx", "head", None),
        P(None, "head", None),
    )
    return jax.shard_map(
        shards,
        mesh=mesh,
        in_specs=placed,
        out_specs=(
            P("ctx", "head", None),
            P("ctx", "head", None),
            P("ctx", "head", None),
            P("ctx", "head"),
            P("ctx", "head"),
            P("ctx", "head", None),
            P("ctx", "head", None),
            P("ctx", "head", None),
            P(("ctx", "head"), None),
        ),
        check_vma=False,
    )
```

```python
import jax
import jax.numpy as jnp
from jax import lax
from jax.sharding import PartitionSpec as P

HOPS = 4


def shortened(x):
    return jax.tree.map(lambda a: a.astype(jnp.bfloat16) if a.dtype == jnp.float32 else a, x)


def from_behind(x, axis, by):
    peers = lax.axis_size(axis)
    pairs = [(i, i + by) for i in range(peers) if 0 <= i + by < peers]
    return lax.ppermute(x, axis, pairs)


def segment_of(positions, doc_starts):
    return jnp.sum((doc_starts[None, :] <= positions[:, None]).astype(jnp.int32), axis=1) - 1


def matmul(spec, a, b):
    return jnp.einsum(spec, a, b, precision=lax.Precision.HIGHEST)


def unit_lower_inverse(lower):
    n = lower.shape[-1]
    rows = jnp.arange(n)[:, None]
    cols = jnp.arange(n)[None, :]
    eye = jnp.eye(n, dtype=jnp.float32)
    first = (rows // 2 == cols // 2) & (rows % 2 == 1) & (cols % 2 == 0)
    inverse = eye - jnp.where(first, lower, 0.0)
    size = 2
    while size < n:
        mask = (rows // (2 * size) == cols // (2 * size)) & ((rows // size) % 2 == 1) & (
            (cols // size) % 2 == 0
        )
        block = jnp.where(mask, lower, 0.0)
        inverse = inverse - matmul("hij,hjk->hik", inverse, matmul("hij,hjk->hik", block, inverse))
        size *= 2
    return inverse


@jax.custom_vjp
def unit_lower_solve(lower, inverse, target):
    return matmul("hts,hsv->htv", inverse, target)


def unit_lower_solve_fwd(lower, inverse, target):
    written = matmul("hts,hsv->htv", inverse, target)
    return written, (inverse, written)


def unit_lower_solve_bwd(saved, grad):
    inverse, written = saved
    target_grad = matmul("hst,hsv->htv", inverse, grad)
    n = inverse.shape[-1]
    strict = jnp.arange(n)[:, None] > jnp.arange(n)[None, :]
    lower_grad = jnp.where(strict, -matmul("htv,hsv->hts", target_grad, written), 0.0)
    return lower_grad, jnp.zeros_like(inverse), target_grad


unit_lower_solve.defvjp(unit_lower_solve_fwd, unit_lower_solve_bwd)


def block_system(key_rows, strength, decay_rows, segment, repeat):
    unit_key = key_rows * lax.rsqrt(jnp.sum(key_rows * key_rows, axis=-1, keepdims=True) + 1e-06)
    unit_key = jnp.repeat(unit_key, repeat, axis=1)
    length = segment.shape[0]
    offsets = jnp.arange(length)
    cumulative = jnp.cumsum(decay_rows, axis=0).T
    same_doc = segment[:, None] == segment[None, :]
    causal = offsets[:, None] >= offsets[None, :]
    strictly = offsets[:, None] > offsets[None, :]
    spread = cumulative[:, :, None] - cumulative[:, None, :]
    inclusive = jnp.exp(jnp.where(same_doc & causal, spread, -jnp.inf))
    exclusive = jnp.where(strictly, inclusive, 0.0)
    key_key = jnp.einsum("thd,shd->hts", unit_key, unit_key, precision=lax.Precision.HIGHEST)
    return strength.T[:, :, None] * key_key * exclusive


def delta_block(
    queries, key_rows, value_rows, strength, decay_rows, start_state, segment, continued, inverse
):
    head_size = queries.shape[-1]
    repeat = value_rows.shape[1] // queries.shape[1]
    highest = lax.Precision.HIGHEST
    unit_query = (
        queries
        * lax.rsqrt(jnp.sum(queries * queries, axis=-1, keepdims=True) + 1e-06)
        * head_size ** (-0.5)
    )
    unit_key = key_rows * lax.rsqrt(jnp.sum(key_rows * key_rows, axis=-1, keepdims=True) + 1e-06)
    unit_query = jnp.repeat(unit_query, repeat, axis=1)
    unit_key = jnp.repeat(unit_key, repeat, axis=1)
    length = segment.shape[0]
    offsets = jnp.arange(length)
    cumulative = jnp.cumsum(decay_rows, axis=0).T
    same_doc = segment[:, None] == segment[None, :]
    causal = offsets[:, None] >= offsets[None, :]
    strictly = offsets[:, None] > offsets[None, :]
    spread = cumulative[:, :, None] - cumulative[:, None, :]
    inclusive = jnp.exp(jnp.where(same_doc & causal, spread, -jnp.inf))
    exclusive = jnp.where(strictly, inclusive, 0.0)
    carried = jnp.exp(cumulative) * continued.astype(jnp.float32)[None, :]
    key_key = jnp.einsum("thd,shd->hts", unit_key, unit_key, precision=highest)
    query_key = jnp.einsum("thd,shd->hts", unit_query, unit_key, precision=highest)
    strength_heads = strength.T
    system = jnp.eye(length, dtype=jnp.float32) + strength_heads[:, :, None] * key_key * exclusive
    recalled = jnp.einsum("thk,hvk->htv", unit_key, start_state, precision=highest)
    target = strength_heads[:, :, None] * (
        value_rows.transpose(1, 0, 2) - carried[:, :, None] * recalled
    )
    written = unit_lower_solve(system - jnp.eye(length, dtype=jnp.float32), inverse, target)
    readout = carried[:, :, None] * jnp.einsum(
        "thk,hvk->htv", unit_query, start_state, precision=highest
    )
    readout = readout + jnp.einsum(
        "hts,hsv->htv", query_key * inclusive, written, precision=highest
    )
    last_doc = segment == segment[-1]
    fading = jnp.exp(jnp.where(last_doc[None, :], cumulative[:, -1:] - cumulative, -jnp.inf))
    final_state = carried[:, -1][:, None, None] * start_state
    final_state = final_state + jnp.einsum(
        "htv,thk->hvk", written * fading[:, :, None], unit_key, precision=highest
    )
    return (readout.transpose(1, 0, 2), final_state)


def carry_back(incoming, mapping):
    return jnp.einsum("hvk,hjk->hvj", incoming, mapping, precision=lax.Precision.HIGHEST)


def shards(
    document_lengths,
    delta_query,
    delta_keys,
    delta_values,
    write_strength,
    log_decay,
    saved_state,
    delta_cotangent,
    soft_query,
    soft_keys,
    soft_values,
    gate_logits,
    soft_cotangent,
    gate_weight,
):
    length = delta_query.shape[0]
    block_index = lax.axis_index("ctx")
    offsets = jnp.arange(length, dtype=jnp.int32)
    doc_starts = jnp.cumsum(document_lengths) - document_lengths
    positions = block_index * length + offsets
    segment = segment_of(positions, doc_starts)
    before = segment_of(positions[:1] - 1, doc_starts)
    continued = segment == before[0]

    local_pair = jnp.stack([soft_keys, soft_values])
    farthest = from_behind(local_pair, "ctx", HOPS)
    near = jnp.concatenate([from_behind(local_pair, "ctx", 1), local_pair], axis=1)
    window_pair = jnp.concatenate([farthest, from_behind(near, "ctx", 2), near], axis=1)

    queries = delta_query.astype(jnp.float32)
    key_rows = delta_keys.astype(jnp.float32)
    value_rows = delta_values.astype(jnp.float32)
    repeat = value_rows.shape[1] // queries.shape[1]
    inverse = lax.stop_gradient(
        unit_lower_inverse(block_system(key_rows, write_strength, log_decay, segment, repeat))
    )
    inverse, window_pair = lax.optimization_barrier((inverse, window_pair))

    kv_heads = soft_keys.shape[1]
    width = soft_keys.shape[2]
    group = soft_query.shape[1] // kv_heads
    score_scale = width ** (-0.5)
    key_positions = (block_index - HOPS) * length + jnp.arange((HOPS + 1) * length, dtype=jnp.int32)
    key_segment = segment_of(key_positions, doc_starts)
    keep = (segment[:, None] == key_segment[None, :]) & (
        key_positions[None, :] <= positions[:, None]
    )
    queries_four = soft_query.reshape(length, kv_heads, group, width)
    scores = (
        jnp.einsum(
            "qkgd,tkd->kgqt", queries_four, window_pair[0], preferred_element_type=jnp.float32
        )
        * score_scale
    )
    scores = jnp.where(keep, scores, -jnp.inf)
    peak = jnp.max(scores, axis=-1, keepdims=True)
    log_total = peak + jnp.log(jnp.sum(jnp.exp(scores - peak), axis=-1, keepdims=True))
    weights = jnp.exp(scores - log_total)
    rounded = weights.astype(jnp.bfloat16)
    output = jnp.einsum(
        "kgqt,tkd->qkgd", rounded, window_pair[1], preferred_element_type=jnp.float32
    )
    gate_open = jax.nn.sigmoid(gate_logits.astype(jnp.float32)).reshape(
        length, kv_heads, group, width
    )
    upstream = soft_cotangent.astype(jnp.float32).reshape(length, kv_heads, group, width)
    slope = (
        (upstream * output * gate_open * (1.0 - gate_open))
        .astype(jnp.bfloat16)
        .reshape(length, kv_heads * group, width)
    )
    gate_full = lax.dot_general(
        slope, gate_weight, (((1, 2), (1, 2)), ((), ())), preferred_element_type=jnp.float32
    )
    gate_part = gate_full.astype(jnp.bfloat16)
    gate_full, gate_part, inverse, queries, key_rows, value_rows = lax.optimization_barrier(
        (gate_full, gate_part, inverse, queries, key_rows, value_rows)
    )
    half = gate_part.shape[0] // 2
    head_index = lax.axis_index("head")
    kept = lax.dynamic_slice_in_dim(gate_full, head_index * half, half, 0)
    sent = lax.dynamic_slice_in_dim(gate_part, (1 - head_index) * half, half, 0)
    received = lax.ppermute(sent, "head", [(0, 1), (1, 0)])

    start_state = saved_state[0]
    cotangent = delta_cotangent.astype(jnp.float32)

    def forward_state(state_in):
        return delta_block(
            queries,
            key_rows,
            value_rows,
            write_strength,
            log_decay,
            state_in,
            segment,
            continued,
            inverse,
        )

    unused_state, state_pullback = jax.vjp(forward_state, start_state)
    own_part = state_pullback((cotangent, jnp.zeros_like(start_state)))[0]
    identity = jnp.broadcast_to(
        jnp.eye(start_state.shape[-1], dtype=jnp.float32), start_state.shape
    )
    transfer = delta_block(
        queries,
        key_rows,
        jnp.zeros_like(value_rows),
        write_strength,
        log_decay,
        identity,
        segment,
        continued,
        inverse,
    )[1]
    back = (upstream * gate_open).astype(jnp.bfloat16)
    row_dot = jnp.sum(back.astype(jnp.float32) * output, axis=-1).transpose(1, 2, 0)[..., None]
    dprob = jnp.einsum("qkgd,tkd->kgqt", back, window_pair[1], preferred_element_type=jnp.float32)
    dscore = (weights * (dprob - row_dot)).astype(jnp.bfloat16)
    query_grad = (
        jnp.einsum("kgqt,tkd->qkgd", dscore, window_pair[0], preferred_element_type=jnp.float32)
        * score_scale
    )
    query_grad = query_grad.reshape(length, kv_heads * group, width)
    key_part = (
        jnp.einsum("kgqt,qkgd->tkd", dscore, queries_four, preferred_element_type=jnp.float32)
        * score_scale
    )
    value_part = jnp.einsum("kgqt,qkgd->tkd", rounded, back, preferred_element_type=jnp.float32)
    lanes = start_state.shape[-1]
    pieces = width // lanes
    returned = (
        jnp.stack([key_part, value_part])
        .reshape(2, HOPS + 1, length, kv_heads, pieces, lanes)
        .transpose(1, 0, 3, 4, 2, 5)
        .reshape(HOPS + 1, 2 * kv_heads * pieces, length, lanes)
    )
    planes = start_state.shape[0]
    gathered = own_part
    incoming = own_part
    summed = returned[0]
    for step_index in range(HOPS):
        payload = jnp.concatenate([shortened(gathered), summed.astype(jnp.bfloat16)], axis=0)
        arrived_back = from_behind(payload, "ctx", -1).astype(jnp.float32)
        incoming = arrived_back[:planes]
        summed = arrived_back[planes:] + returned[step_index + 1]
        gathered = own_part + carry_back(incoming, transfer)
    summed = (
        summed.reshape(2, kv_heads, pieces, length, lanes)
        .transpose(0, 3, 1, 2, 4)
        .reshape(2, length, kv_heads, width)
    )

    received, incoming = lax.optimization_barrier((received, incoming))
    input_grad = kept + received.astype(jnp.float32)

    def forward(queries_in, keys_in, values_in, strength_in, decay_in):
        return delta_block(
            queries_in,
            keys_in,
            values_in,
            strength_in,
            decay_in,
            start_state,
            segment,
            continued,
            inverse,
        )

    unused, pullback = jax.vjp(forward, queries, key_rows, value_rows, write_strength, log_decay)
    readout_grad, address_grad, content_grad, strength_grad, decay_grad = pullback(
        (cotangent, incoming)
    )

    return (
        readout_grad,
        address_grad,
        content_grad,
        strength_grad,
        decay_grad,
        query_grad,
        summed[0],
        summed[1],
        input_grad,
    )


def solution(mesh):
    placed = (
        P(),
        P("ctx", "head", None),
        P("ctx", "head", None),
        P("ctx", "head", None),
        P("ctx", "head"),
        P("ctx", "head"),
        P("ctx", "head", None, None),
        P("ctx", "head", None),
        P("ctx", "head", None),
        P("ctx", "head", None),
        P("ctx", "head", None),
        P("ctx", "head", None),
        P("ctx", "head", None),
        P(None, "head", None),
    )
    return jax.shard_map(
        shards,
        mesh=mesh,
        in_specs=placed,
        out_specs=(
            P("ctx", "head", None),
            P("ctx", "head", None),
            P("ctx", "head", None),
            P("ctx", "head"),
            P("ctx", "head"),
            P("ctx", "head", None),
            P("ctx", "head", None),
            P("ctx", "head", None),
            P(("ctx", "head"), None),
        ),
        check_vma=False,
    )
```

```python
import jax
import jax.numpy as jnp
from jax import lax
from jax.sharding import PartitionSpec as P

HOPS = 4


def shortened(x):
    return jax.tree.map(lambda a: a.astype(jnp.bfloat16) if a.dtype == jnp.float32 else a, x)


def from_behind(x, axis, by):
    peers = lax.axis_size(axis)
    pairs = [(i, i + by) for i in range(peers) if 0 <= i + by < peers]
    return lax.ppermute(x, axis, pairs)


def segment_of(positions, doc_starts):
    return jnp.sum((doc_starts[None, :] <= positions[:, None]).astype(jnp.int32), axis=1) - 1


def matmul(spec, a, b):
    return jnp.einsum(spec, a, b, precision=lax.Precision.HIGHEST)


def unit_lower_inverse(lower):
    n = lower.shape[-1]
    rows = jnp.arange(n)[:, None]
    cols = jnp.arange(n)[None, :]
    eye = jnp.eye(n, dtype=jnp.float32)
    first = (rows // 2 == cols // 2) & (rows % 2 == 1) & (cols % 2 == 0)
    inverse = eye - jnp.where(first, lower, 0.0)
    size = 2
    while size < n:
        mask = (rows // (2 * size) == cols // (2 * size)) & ((rows // size) % 2 == 1) & (
            (cols // size) % 2 == 0
        )
        block = jnp.where(mask, lower, 0.0)
        inverse = inverse - matmul("hij,hjk->hik", inverse, matmul("hij,hjk->hik", block, inverse))
        size *= 2
    return inverse


@jax.custom_vjp
def unit_lower_solve(lower, inverse, target):
    return matmul("hts,hsv->htv", inverse, target)


def unit_lower_solve_fwd(lower, inverse, target):
    written = matmul("hts,hsv->htv", inverse, target)
    return written, (inverse, written)


def unit_lower_solve_bwd(saved, grad):
    inverse, written = saved
    target_grad = matmul("hst,hsv->htv", inverse, grad)
    n = inverse.shape[-1]
    strict = jnp.arange(n)[:, None] > jnp.arange(n)[None, :]
    lower_grad = jnp.where(strict, -matmul("htv,hsv->hts", target_grad, written), 0.0)
    return lower_grad, jnp.zeros_like(inverse), target_grad


unit_lower_solve.defvjp(unit_lower_solve_fwd, unit_lower_solve_bwd)


def block_system(key_rows, strength, decay_rows, segment, repeat):
    unit_key = key_rows * lax.rsqrt(jnp.sum(key_rows * key_rows, axis=-1, keepdims=True) + 1e-06)
    unit_key = jnp.repeat(unit_key, repeat, axis=1)
    length = segment.shape[0]
    offsets = jnp.arange(length)
    cumulative = jnp.cumsum(decay_rows, axis=0).T
    same_doc = segment[:, None] == segment[None, :]
    causal = offsets[:, None] >= offsets[None, :]
    strictly = offsets[:, None] > offsets[None, :]
    spread = cumulative[:, :, None] - cumulative[:, None, :]
    inclusive = jnp.exp(jnp.where(same_doc & causal, spread, -jnp.inf))
    exclusive = jnp.where(strictly, inclusive, 0.0)
    key_key = jnp.einsum("thd,shd->hts", unit_key, unit_key, precision=lax.Precision.HIGHEST)
    return strength.T[:, :, None] * key_key * exclusive


def delta_block(
    queries, key_rows, value_rows, strength, decay_rows, start_state, segment, continued, inverse
):
    head_size = queries.shape[-1]
    repeat = value_rows.shape[1] // queries.shape[1]
    highest = lax.Precision.HIGHEST
    unit_query = (
        queries
        * lax.rsqrt(jnp.sum(queries * queries, axis=-1, keepdims=True) + 1e-06)
        * head_size ** (-0.5)
    )
    unit_key = key_rows * lax.rsqrt(jnp.sum(key_rows * key_rows, axis=-1, keepdims=True) + 1e-06)
    unit_query = jnp.repeat(unit_query, repeat, axis=1)
    unit_key = jnp.repeat(unit_key, repeat, axis=1)
    length = segment.shape[0]
    offsets = jnp.arange(length)
    cumulative = jnp.cumsum(decay_rows, axis=0).T
    same_doc = segment[:, None] == segment[None, :]
    causal = offsets[:, None] >= offsets[None, :]
    strictly = offsets[:, None] > offsets[None, :]
    spread = cumulative[:, :, None] - cumulative[:, None, :]
    inclusive = jnp.exp(jnp.where(same_doc & causal, spread, -jnp.inf))
    exclusive = jnp.where(strictly, inclusive, 0.0)
    carried = jnp.exp(cumulative) * continued.astype(jnp.float32)[None, :]
    key_key = jnp.einsum("thd,shd->hts", unit_key, unit_key, precision=highest)
    query_key = jnp.einsum("thd,shd->hts", unit_query, unit_key, precision=highest)
    strength_heads = strength.T
    system = jnp.eye(length, dtype=jnp.float32) + strength_heads[:, :, None] * key_key * exclusive
    recalled = jnp.einsum("thk,hvk->htv", unit_key, start_state, precision=highest)
    target = strength_heads[:, :, None] * (
        value_rows.transpose(1, 0, 2) - carried[:, :, None] * recalled
    )
    written = unit_lower_solve(system - jnp.eye(length, dtype=jnp.float32), inverse, target)
    readout = carried[:, :, None] * jnp.einsum(
        "thk,hvk->htv", unit_query, start_state, precision=highest
    )
    readout = readout + jnp.einsum(
        "hts,hsv->htv", query_key * inclusive, written, precision=highest
    )
    last_doc = segment == segment[-1]
    fading = jnp.exp(jnp.where(last_doc[None, :], cumulative[:, -1:] - cumulative, -jnp.inf))
    final_state = carried[:, -1][:, None, None] * start_state
    final_state = final_state + jnp.einsum(
        "htv,thk->hvk", written * fading[:, :, None], unit_key, precision=highest
    )
    return (readout.transpose(1, 0, 2), final_state)


def carry_back(incoming, mapping):
    return jnp.einsum("hvk,hjk->hvj", incoming, mapping, precision=lax.Precision.HIGHEST)


def shards(
    document_lengths,
    delta_query,
    delta_keys,
    delta_values,
    write_strength,
    log_decay,
    saved_state,
    delta_cotangent,
    soft_query,
    soft_keys,
    soft_values,
    gate_logits,
    soft_cotangent,
    gate_weight,
):
    length = delta_query.shape[0]
    block_index = lax.axis_index("ctx")
    offsets = jnp.arange(length, dtype=jnp.int32)
    doc_starts = jnp.cumsum(document_lengths) - document_lengths
    positions = block_index * length + offsets
    segment = segment_of(positions, doc_starts)
    before = segment_of(positions[:1] - 1, doc_starts)
    continued = segment == before[0]

    local_pair = jnp.stack([soft_keys, soft_values])
    arrived = [local_pair] + [from_behind(local_pair, "ctx", d) for d in range(1, HOPS + 1)]
    window_pair = jnp.concatenate(arrived[::-1], axis=1)

    queries = delta_query.astype(jnp.float32)
    key_rows = delta_keys.astype(jnp.float32)
    value_rows = delta_values.astype(jnp.float32)
    repeat = value_rows.shape[1] // queries.shape[1]
    inverse = lax.stop_gradient(
        unit_lower_inverse(block_system(key_rows, write_strength, log_decay, segment, repeat))
    )
    inverse, window_pair = lax.optimization_barrier((inverse, window_pair))

    kv_heads = soft_keys.shape[1]
    width = soft_keys.shape[2]
    group = soft_query.shape[1] // kv_heads
    score_scale = width ** (-0.5)
    key_positions = (block_index - HOPS) * length + jnp.arange((HOPS + 1) * length, dtype=jnp.int32)
    key_segment = segment_of(key_positions, doc_starts)
    keep = (segment[:, None] == key_segment[None, :]) & (
        key_positions[None, :] <= positions[:, None]
    )
    queries_four = soft_query.reshape(length, kv_heads, group, width)
    scores = (
        jnp.einsum(
            "qkgd,tkd->kgqt", queries_four, window_pair[0], preferred_element_type=jnp.float32
        )
        * score_scale
    )
    scores = jnp.where(keep, scores, -jnp.inf)
    peak = jnp.max(scores, axis=-1, keepdims=True)
    log_total = peak + jnp.log(jnp.sum(jnp.exp(scores - peak), axis=-1, keepdims=True))
    weights = jnp.exp(scores - log_total)
    rounded = weights.astype(jnp.bfloat16)
    output = jnp.einsum(
        "kgqt,tkd->qkgd", rounded, window_pair[1], preferred_element_type=jnp.float32
    )
    gate_open = jax.nn.sigmoid(gate_logits.astype(jnp.float32)).reshape(
        length, kv_heads, group, width
    )
    upstream = soft_cotangent.astype(jnp.float32).reshape(length, kv_heads, group, width)
    slope = (
        (upstream * output * gate_open * (1.0 - gate_open))
        .astype(jnp.bfloat16)
        .reshape(length, kv_heads * group, width)
    )
    gate_full = lax.dot_general(
        slope, gate_weight, (((1, 2), (1, 2)), ((), ())), preferred_element_type=jnp.float32
    )
    gate_part = gate_full.astype(jnp.bfloat16)
    gate_full, gate_part, inverse, queries, key_rows, value_rows = lax.optimization_barrier(
        (gate_full, gate_part, inverse, queries, key_rows, value_rows)
    )
    half = gate_part.shape[0] // 2
    head_index = lax.axis_index("head")
    kept = lax.dynamic_slice_in_dim(gate_full, head_index * half, half, 0)
    sent = lax.dynamic_slice_in_dim(gate_part, (1 - head_index) * half, half, 0)
    received = lax.ppermute(sent, "head", [(0, 1), (1, 0)])

    start_state = saved_state[0]
    cotangent = delta_cotangent.astype(jnp.float32)

    def forward_state(state_in):
        return delta_block(
            queries,
            key_rows,
            value_rows,
            write_strength,
            log_decay,
            state_in,
            segment,
            continued,
            inverse,
        )

    unused_state, state_pullback = jax.vjp(forward_state, start_state)
    own_part = state_pullback((cotangent, jnp.zeros_like(start_state)))[0]
    identity = jnp.broadcast_to(
        jnp.eye(start_state.shape[-1], dtype=jnp.float32), start_state.shape
    )
    transfer = delta_block(
        queries,
        key_rows,
        jnp.zeros_like(value_rows),
        write_strength,
        log_decay,
        identity,
        segment,
        continued,
        inverse,
    )[1]
    back = (upstream * gate_open).astype(jnp.bfloat16)
    row_dot = jnp.sum(back.astype(jnp.float32) * output, axis=-1).transpose(1, 2, 0)[..., None]
    dprob = jnp.einsum("qkgd,tkd->kgqt", back, window_pair[1], preferred_element_type=jnp.float32)
    dscore = (weights * (dprob - row_dot)).astype(jnp.bfloat16)
    query_grad = (
        jnp.einsum("kgqt,tkd->qkgd", dscore, window_pair[0], preferred_element_type=jnp.float32)
        * score_scale
    )
    query_grad = query_grad.reshape(length, kv_heads * group, width)
    key_part = (
        jnp.einsum("kgqt,qkgd->tkd", dscore, queries_four, preferred_element_type=jnp.float32)
        * score_scale
    )
    value_part = jnp.einsum("kgqt,qkgd->tkd", rounded, back, preferred_element_type=jnp.float32)
    lanes = start_state.shape[-1]
    pieces = width // lanes
    returned = (
        jnp.stack([key_part, value_part])
        .reshape(2, HOPS + 1, length, kv_heads, pieces, lanes)
        .transpose(1, 0, 3, 4, 2, 5)
        .reshape(HOPS + 1, 2 * kv_heads * pieces, length, lanes)
    )
    planes = start_state.shape[0]
    gathered = own_part
    incoming = own_part
    summed = returned[0]
    for step_index in range(HOPS):
        payload = jnp.concatenate([shortened(gathered), summed.astype(jnp.bfloat16)], axis=0)
        arrived_back = from_behind(payload, "ctx", -1).astype(jnp.float32)
        incoming = arrived_back[:planes]
        summed = arrived_back[planes:] + returned[step_index + 1]
        gathered = own_part + carry_back(incoming, transfer)
    summed = (
        summed.reshape(2, kv_heads, pieces, length, lanes)
        .transpose(0, 3, 1, 2, 4)
        .reshape(2, length, kv_heads, width)
    )

    received, incoming = lax.optimization_barrier((received, incoming))
    input_grad = kept + received.astype(jnp.float32)

    def forward(queries_in, keys_in, values_in, strength_in, decay_in):
        return delta_block(
            queries_in,
            keys_in,
            values_in,
            strength_in,
            decay_in,
            start_state,
            segment,
            continued,
            inverse,
        )

    unused, pullback = jax.vjp(forward, queries, key_rows, value_rows, write_strength, log_decay)
    readout_grad, address_grad, content_grad, strength_grad, decay_grad = pullback(
        (cotangent, incoming)
    )

    return (
        readout_grad,
        address_grad,
        content_grad,
        strength_grad,
        decay_grad,
        query_grad,
        summed[0],
        summed[1],
        input_grad,
    )


def solution(mesh):
    placed = (
        P(),
        P("ctx", "head", None),
        P("ctx", "head", None),
        P("ctx", "head", None),
        P("ctx", "head"),
        P("ctx", "head"),
        P("ctx", "head", None, None),
        P("ctx", "head", None),
        P("ctx", "head", None),
        P("ctx", "head", None),
        P("ctx", "head", None),
        P("ctx", "head", None),
        P("ctx", "head", None),
        P(None, "head", None),
    )
    return jax.shard_map(
        shards,
        mesh=mesh,
        in_specs=placed,
        out_specs=(
            P("ctx", "head", None),
            P("ctx", "head", None),
            P("ctx", "head", None),
            P("ctx", "head"),
            P("ctx", "head"),
            P("ctx", "head", None),
            P("ctx", "head", None),
            P("ctx", "head", None),
            P(("ctx", "head"), None),
        ),
        check_vma=False,
    )
```

```python
import jax
import jax.numpy as jnp
from jax import lax
from jax.sharding import PartitionSpec as P

HOPS = 4


def shortened(x):
    return jax.tree.map(lambda a: a.astype(jnp.bfloat16) if a.dtype == jnp.float32 else a, x)


def from_behind(x, axis, by):
    peers = lax.axis_size(axis)
    pairs = [(i, i + by) for i in range(peers) if 0 <= i + by < peers]
    return lax.ppermute(x, axis, pairs)


def segment_of(positions, doc_starts):
    return jnp.sum((doc_starts[None, :] <= positions[:, None]).astype(jnp.int32), axis=1) - 1


def matmul(spec, a, b):
    return jnp.einsum(spec, a, b, precision=lax.Precision.HIGH)


def unit_lower_inverse(lower):
    n = lower.shape[-1]
    rows = jnp.arange(n)[:, None]
    cols = jnp.arange(n)[None, :]
    eye = jnp.eye(n, dtype=jnp.float32)
    first = (rows // 2 == cols // 2) & (rows % 2 == 1) & (cols % 2 == 0)
    inverse = eye - jnp.where(first, lower, 0.0)
    size = 2
    while size < n:
        mask = (rows // (2 * size) == cols // (2 * size)) & ((rows // size) % 2 == 1) & (
            (cols // size) % 2 == 0
        )
        block = jnp.where(mask, lower, 0.0)
        inverse = inverse - matmul("hij,hjk->hik", inverse, matmul("hij,hjk->hik", block, inverse))
        size *= 2
    return inverse


@jax.custom_vjp
def unit_lower_solve(lower, inverse, target):
    return matmul("hts,hsv->htv", inverse, target)


def unit_lower_solve_fwd(lower, inverse, target):
    written = matmul("hts,hsv->htv", inverse, target)
    return written, (inverse, written)


def unit_lower_solve_bwd(saved, grad):
    inverse, written = saved
    target_grad = matmul("hst,hsv->htv", inverse, grad)
    n = inverse.shape[-1]
    strict = jnp.arange(n)[:, None] > jnp.arange(n)[None, :]
    lower_grad = jnp.where(strict, -matmul("htv,hsv->hts", target_grad, written), 0.0)
    return lower_grad, jnp.zeros_like(inverse), target_grad


unit_lower_solve.defvjp(unit_lower_solve_fwd, unit_lower_solve_bwd)


def block_system(key_rows, strength, decay_rows, segment, repeat):
    unit_key = key_rows * lax.rsqrt(jnp.sum(key_rows * key_rows, axis=-1, keepdims=True) + 1e-06)
    unit_key = jnp.repeat(unit_key, repeat, axis=1)
    length = segment.shape[0]
    offsets = jnp.arange(length)
    cumulative = jnp.cumsum(decay_rows, axis=0).T
    same_doc = segment[:, None] == segment[None, :]
    causal = offsets[:, None] >= offsets[None, :]
    strictly = offsets[:, None] > offsets[None, :]
    spread = cumulative[:, :, None] - cumulative[:, None, :]
    inclusive = jnp.exp(jnp.where(same_doc & causal, spread, -jnp.inf))
    exclusive = jnp.where(strictly, inclusive, 0.0)
    key_key = jnp.einsum("thd,shd->hts", unit_key, unit_key, precision=lax.Precision.HIGH)
    return strength.T[:, :, None] * key_key * exclusive


def delta_block(
    queries, key_rows, value_rows, strength, decay_rows, start_state, segment, continued, inverse
):
    head_size = queries.shape[-1]
    repeat = value_rows.shape[1] // queries.shape[1]
    highest = lax.Precision.HIGH
    unit_query = (
        queries
        * lax.rsqrt(jnp.sum(queries * queries, axis=-1, keepdims=True) + 1e-06)
        * head_size ** (-0.5)
    )
    unit_key = key_rows * lax.rsqrt(jnp.sum(key_rows * key_rows, axis=-1, keepdims=True) + 1e-06)
    unit_query = jnp.repeat(unit_query, repeat, axis=1)
    unit_key = jnp.repeat(unit_key, repeat, axis=1)
    length = segment.shape[0]
    offsets = jnp.arange(length)
    cumulative = jnp.cumsum(decay_rows, axis=0).T
    same_doc = segment[:, None] == segment[None, :]
    causal = offsets[:, None] >= offsets[None, :]
    strictly = offsets[:, None] > offsets[None, :]
    spread = cumulative[:, :, None] - cumulative[:, None, :]
    inclusive = jnp.exp(jnp.where(same_doc & causal, spread, -jnp.inf))
    exclusive = jnp.where(strictly, inclusive, 0.0)
    carried = jnp.exp(cumulative) * continued.astype(jnp.float32)[None, :]
    key_key = jnp.einsum("thd,shd->hts", unit_key, unit_key, precision=highest)
    query_key = jnp.einsum("thd,shd->hts", unit_query, unit_key, precision=highest)
    strength_heads = strength.T
    system = jnp.eye(length, dtype=jnp.float32) + strength_heads[:, :, None] * key_key * exclusive
    recalled = jnp.einsum("thk,hvk->htv", unit_key, start_state, precision=highest)
    target = strength_heads[:, :, None] * (
        value_rows.transpose(1, 0, 2) - carried[:, :, None] * recalled
    )
    written = unit_lower_solve(system - jnp.eye(length, dtype=jnp.float32), inverse, target)
    readout = carried[:, :, None] * jnp.einsum(
        "thk,hvk->htv", unit_query, start_state, precision=highest
    )
    readout = readout + jnp.einsum(
        "hts,hsv->htv", query_key * inclusive, written, precision=highest
    )
    last_doc = segment == segment[-1]
    fading = jnp.exp(jnp.where(last_doc[None, :], cumulative[:, -1:] - cumulative, -jnp.inf))
    final_state = carried[:, -1][:, None, None] * start_state
    final_state = final_state + jnp.einsum(
        "htv,thk->hvk", written * fading[:, :, None], unit_key, precision=highest
    )
    return (readout.transpose(1, 0, 2), final_state)


def carry_back(incoming, mapping):
    return jnp.einsum("hvk,hjk->hvj", incoming, mapping, precision=lax.Precision.HIGH)


def shards(
    document_lengths,
    delta_query,
    delta_keys,
    delta_values,
    write_strength,
    log_decay,
    saved_state,
    delta_cotangent,
    soft_query,
    soft_keys,
    soft_values,
    gate_logits,
    soft_cotangent,
    gate_weight,
):
    length = delta_query.shape[0]
    block_index = lax.axis_index("ctx")
    offsets = jnp.arange(length, dtype=jnp.int32)
    doc_starts = jnp.cumsum(document_lengths) - document_lengths
    positions = block_index * length + offsets
    segment = segment_of(positions, doc_starts)
    before = segment_of(positions[:1] - 1, doc_starts)
    continued = segment == before[0]

    local_pair = jnp.stack([soft_keys, soft_values])
    arrived = [local_pair] + [from_behind(local_pair, "ctx", d) for d in range(1, HOPS + 1)]
    window_pair = jnp.concatenate(arrived[::-1], axis=1)

    queries = delta_query.astype(jnp.float32)
    key_rows = delta_keys.astype(jnp.float32)
    value_rows = delta_values.astype(jnp.float32)
    repeat = value_rows.shape[1] // queries.shape[1]
    inverse = lax.stop_gradient(
        unit_lower_inverse(block_system(key_rows, write_strength, log_decay, segment, repeat))
    )
    inverse, window_pair = lax.optimization_barrier((inverse, window_pair))

    kv_heads = soft_keys.shape[1]
    width = soft_keys.shape[2]
    group = soft_query.shape[1] // kv_heads
    score_scale = width ** (-0.5)
    key_positions = (block_index - HOPS) * length + jnp.arange((HOPS + 1) * length, dtype=jnp.int32)
    key_segment = segment_of(key_positions, doc_starts)
    keep = (segment[:, None] == key_segment[None, :]) & (
        key_positions[None, :] <= positions[:, None]
    )
    queries_four = soft_query.reshape(length, kv_heads, group, width)
    scores = (
        jnp.einsum(
            "qkgd,tkd->kgqt", queries_four, window_pair[0], preferred_element_type=jnp.float32
        )
        * score_scale
    )
    scores = jnp.where(keep, scores, -jnp.inf)
    peak = jnp.max(scores, axis=-1, keepdims=True)
    log_total = peak + jnp.log(jnp.sum(jnp.exp(scores - peak), axis=-1, keepdims=True))
    weights = jnp.exp(scores - log_total)
    rounded = weights.astype(jnp.bfloat16)
    output = jnp.einsum(
        "kgqt,tkd->qkgd", rounded, window_pair[1], preferred_element_type=jnp.float32
    )
    gate_open = jax.nn.sigmoid(gate_logits.astype(jnp.float32)).reshape(
        length, kv_heads, group, width
    )
    upstream = soft_cotangent.astype(jnp.float32).reshape(length, kv_heads, group, width)
    slope = (
        (upstream * output * gate_open * (1.0 - gate_open))
        .astype(jnp.bfloat16)
        .reshape(length, kv_heads * group, width)
    )
    gate_full = lax.dot_general(
        slope, gate_weight, (((1, 2), (1, 2)), ((), ())), preferred_element_type=jnp.float32
    )
    gate_part = gate_full.astype(jnp.bfloat16)
    gate_full, gate_part, inverse, queries, key_rows, value_rows = lax.optimization_barrier(
        (gate_full, gate_part, inverse, queries, key_rows, value_rows)
    )
    half = gate_part.shape[0] // 2
    head_index = lax.axis_index("head")
    kept = lax.dynamic_slice_in_dim(gate_full, head_index * half, half, 0)
    sent = lax.dynamic_slice_in_dim(gate_part, (1 - head_index) * half, half, 0)
    received = lax.ppermute(sent, "head", [(0, 1), (1, 0)])

    start_state = saved_state[0]
    cotangent = delta_cotangent.astype(jnp.float32)

    def forward_state(state_in):
        return delta_block(
            queries,
            key_rows,
            value_rows,
            write_strength,
            log_decay,
            state_in,
            segment,
            continued,
            inverse,
        )

    unused_state, state_pullback = jax.vjp(forward_state, start_state)
    own_part = state_pullback((cotangent, jnp.zeros_like(start_state)))[0]
    identity = jnp.broadcast_to(
        jnp.eye(start_state.shape[-1], dtype=jnp.float32), start_state.shape
    )
    transfer = delta_block(
        queries,
        key_rows,
        jnp.zeros_like(value_rows),
        write_strength,
        log_decay,
        identity,
        segment,
        continued,
        inverse,
    )[1]
    gathered = own_part
    incoming = own_part
    for step_index in range(HOPS):
        incoming = from_behind(shortened(gathered), "ctx", -1).astype(gathered.dtype)
        gathered = own_part + carry_back(incoming, transfer)

    received, incoming = lax.optimization_barrier((received, incoming))
    input_grad = kept + received.astype(jnp.float32)

    def forward(queries_in, keys_in, values_in, strength_in, decay_in):
        return delta_block(
            queries_in,
            keys_in,
            values_in,
            strength_in,
            decay_in,
            start_state,
            segment,
            continued,
            inverse,
        )

    unused, pullback = jax.vjp(forward, queries, key_rows, value_rows, write_strength, log_decay)
    readout_grad, address_grad, content_grad, strength_grad, decay_grad = pullback(
        (cotangent, incoming)
    )

    back = (upstream * gate_open).astype(jnp.bfloat16)
    row_dot = jnp.sum(back.astype(jnp.float32) * output, axis=-1).transpose(1, 2, 0)[..., None]
    dprob = jnp.einsum("qkgd,tkd->kgqt", back, window_pair[1], preferred_element_type=jnp.float32)
    dscore = (weights * (dprob - row_dot)).astype(jnp.bfloat16)
    query_grad = (
        jnp.einsum("kgqt,tkd->qkgd", dscore, window_pair[0], preferred_element_type=jnp.float32)
        * score_scale
    )
    query_grad = query_grad.reshape(length, kv_heads * group, width)
    key_part = (
        jnp.einsum("kgqt,qkgd->tkd", dscore, queries_four, preferred_element_type=jnp.float32)
        * score_scale
    )
    value_part = jnp.einsum("kgqt,qkgd->tkd", rounded, back, preferred_element_type=jnp.float32)
    returned = jnp.stack([key_part, value_part])

    def slab(distance):
        return returned[:, (HOPS - distance) * length : (HOPS - distance + 1) * length]

    summed = slab(0)
    for distance in range(1, HOPS + 1):
        summed = summed + from_behind(
            slab(distance).astype(jnp.bfloat16), "ctx", -distance
        ).astype(summed.dtype)
    return (
        readout_grad,
        address_grad,
        content_grad,
        strength_grad,
        decay_grad,
        query_grad,
        summed[0],
        summed[1],
        input_grad,
    )


def solution(mesh):
    placed = (
        P(),
        P("ctx", "head", None),
        P("ctx", "head", None),
        P("ctx", "head", None),
        P("ctx", "head"),
        P("ctx", "head"),
        P("ctx", "head", None, None),
        P("ctx", "head", None),
        P("ctx", "head", None),
        P("ctx", "head", None),
        P("ctx", "head", None),
        P("ctx", "head", None),
        P("ctx", "head", None),
        P(None, "head", None),
    )
    return jax.shard_map(
        shards,
        mesh=mesh,
        in_specs=placed,
        out_specs=(
            P("ctx", "head", None),
            P("ctx", "head", None),
            P("ctx", "head", None),
            P("ctx", "head"),
            P("ctx", "head"),
            P("ctx", "head", None),
            P("ctx", "head", None),
            P("ctx", "head", None),
            P(("ctx", "head"), None),
        ),
        check_vma=False,
    )
```

```python
import jax
import jax.numpy as jnp
from jax import lax
from jax.sharding import PartitionSpec as P

HOPS = 4


def shortened(x):
    return jax.tree.map(lambda a: a.astype(jnp.bfloat16) if a.dtype == jnp.float32 else a, x)


def from_behind(x, axis, by):
    peers = lax.axis_size(axis)
    pairs = [(i, i + by) for i in range(peers) if 0 <= i + by < peers]
    return lax.ppermute(x, axis, pairs)


def segment_of(positions, doc_starts):
    return jnp.sum((doc_starts[None, :] <= positions[:, None]).astype(jnp.int32), axis=1) - 1


def matmul(spec, a, b):
    return jnp.einsum(spec, a, b, precision=lax.Precision.HIGH)


def unit_lower_inverse(lower):
    n = lower.shape[-1]
    rows = jnp.arange(n)[:, None]
    cols = jnp.arange(n)[None, :]
    eye = jnp.eye(n, dtype=jnp.float32)
    first = (rows // 2 == cols // 2) & (rows % 2 == 1) & (cols % 2 == 0)
    inverse = eye - jnp.where(first, lower, 0.0)
    size = 2
    while size < n:
        mask = (rows // (2 * size) == cols // (2 * size)) & ((rows // size) % 2 == 1) & (
            (cols // size) % 2 == 0
        )
        block = jnp.where(mask, lower, 0.0)
        inverse = inverse - matmul("hij,hjk->hik", inverse, matmul("hij,hjk->hik", block, inverse))
        size *= 2
    return inverse


@jax.custom_vjp
def unit_lower_solve(lower, inverse, target):
    return matmul("hts,hsv->htv", inverse, target)


def unit_lower_solve_fwd(lower, inverse, target):
    written = matmul("hts,hsv->htv", inverse, target)
    return written, (inverse, written)


def unit_lower_solve_bwd(saved, grad):
    inverse, written = saved
    target_grad = matmul("hst,hsv->htv", inverse, grad)
    n = inverse.shape[-1]
    strict = jnp.arange(n)[:, None] > jnp.arange(n)[None, :]
    lower_grad = jnp.where(strict, -matmul("htv,hsv->hts", target_grad, written), 0.0)
    return lower_grad, jnp.zeros_like(inverse), target_grad


unit_lower_solve.defvjp(unit_lower_solve_fwd, unit_lower_solve_bwd)


def block_system(key_rows, strength, decay_rows, segment, repeat):
    unit_key = key_rows * lax.rsqrt(jnp.sum(key_rows * key_rows, axis=-1, keepdims=True) + 1e-06)
    unit_key = jnp.repeat(unit_key, repeat, axis=1)
    length = segment.shape[0]
    offsets = jnp.arange(length)
    cumulative = jnp.cumsum(decay_rows, axis=0).T
    same_doc = segment[:, None] == segment[None, :]
    causal = offsets[:, None] >= offsets[None, :]
    strictly = offsets[:, None] > offsets[None, :]
    spread = cumulative[:, :, None] - cumulative[:, None, :]
    inclusive = jnp.exp(jnp.where(same_doc & causal, spread, -jnp.inf))
    exclusive = jnp.where(strictly, inclusive, 0.0)
    key_key = jnp.einsum("thd,shd->hts", unit_key, unit_key, precision=lax.Precision.HIGH)
    return strength.T[:, :, None] * key_key * exclusive


def delta_block(
    queries, key_rows, value_rows, strength, decay_rows, start_state, segment, continued, inverse
):
    head_size = queries.shape[-1]
    repeat = value_rows.shape[1] // queries.shape[1]
    highest = lax.Precision.HIGH
    unit_query = (
        queries
        * lax.rsqrt(jnp.sum(queries * queries, axis=-1, keepdims=True) + 1e-06)
        * head_size ** (-0.5)
    )
    unit_key = key_rows * lax.rsqrt(jnp.sum(key_rows * key_rows, axis=-1, keepdims=True) + 1e-06)
    unit_query = jnp.repeat(unit_query, repeat, axis=1)
    unit_key = jnp.repeat(unit_key, repeat, axis=1)
    length = segment.shape[0]
    offsets = jnp.arange(length)
    cumulative = jnp.cumsum(decay_rows, axis=0).T
    same_doc = segment[:, None] == segment[None, :]
    causal = offsets[:, None] >= offsets[None, :]
    strictly = offsets[:, None] > offsets[None, :]
    spread = cumulative[:, :, None] - cumulative[:, None, :]
    inclusive = jnp.exp(jnp.where(same_doc & causal, spread, -jnp.inf))
    exclusive = jnp.where(strictly, inclusive, 0.0)
    carried = jnp.exp(cumulative) * continued.astype(jnp.float32)[None, :]
    key_key = jnp.einsum("thd,shd->hts", unit_key, unit_key, precision=highest)
    query_key = jnp.einsum("thd,shd->hts", unit_query, unit_key, precision=highest)
    strength_heads = strength.T
    system = jnp.eye(length, dtype=jnp.float32) + strength_heads[:, :, None] * key_key * exclusive
    recalled = jnp.einsum("thk,hvk->htv", unit_key, start_state, precision=highest)
    target = strength_heads[:, :, None] * (
        value_rows.transpose(1, 0, 2) - carried[:, :, None] * recalled
    )
    written = unit_lower_solve(system - jnp.eye(length, dtype=jnp.float32), inverse, target)
    readout = carried[:, :, None] * jnp.einsum(
        "thk,hvk->htv", unit_query, start_state, precision=highest
    )
    readout = readout + jnp.einsum(
        "hts,hsv->htv", query_key * inclusive, written, precision=highest
    )
    last_doc = segment == segment[-1]
    fading = jnp.exp(jnp.where(last_doc[None, :], cumulative[:, -1:] - cumulative, -jnp.inf))
    final_state = carried[:, -1][:, None, None] * start_state
    final_state = final_state + jnp.einsum(
        "htv,thk->hvk", written * fading[:, :, None], unit_key, precision=highest
    )
    return (readout.transpose(1, 0, 2), final_state)


def carry_back(incoming, mapping):
    return jnp.einsum("hvk,hjk->hvj", incoming, mapping, precision=lax.Precision.HIGH)


def shards(
    document_lengths,
    delta_query,
    delta_keys,
    delta_values,
    write_strength,
    log_decay,
    saved_state,
    delta_cotangent,
    soft_query,
    soft_keys,
    soft_values,
    gate_logits,
    soft_cotangent,
    gate_weight,
):
    length = delta_query.shape[0]
    block_index = lax.axis_index("ctx")
    offsets = jnp.arange(length, dtype=jnp.int32)
    doc_starts = jnp.cumsum(document_lengths) - document_lengths
    positions = block_index * length + offsets
    segment = segment_of(positions, doc_starts)
    before = segment_of(positions[:1] - 1, doc_starts)
    continued = segment == before[0]

    local_pair = jnp.stack([soft_keys, soft_values])
    arrived = [local_pair] + [from_behind(local_pair, "ctx", d) for d in range(1, HOPS + 1)]
    window_pair = jnp.concatenate(arrived[::-1], axis=1)

    queries = delta_query.astype(jnp.float32)
    key_rows = delta_keys.astype(jnp.float32)
    value_rows = delta_values.astype(jnp.float32)
    repeat = value_rows.shape[1] // queries.shape[1]
    inverse = lax.stop_gradient(
        unit_lower_inverse(block_system(key_rows, write_strength, log_decay, segment, repeat))
    )

    kv_heads = soft_keys.shape[1]
    width = soft_keys.shape[2]
    group = soft_query.shape[1] // kv_heads
    score_scale = width ** (-0.5)
    key_positions = (block_index - HOPS) * length + jnp.arange((HOPS + 1) * length, dtype=jnp.int32)
    key_segment = segment_of(key_positions, doc_starts)
    keep = (segment[:, None] == key_segment[None, :]) & (
        key_positions[None, :] <= positions[:, None]
    )
    queries_four = soft_query.reshape(length, kv_heads, group, width)
    scores = (
        jnp.einsum(
            "qkgd,tkd->kgqt", queries_four, window_pair[0], preferred_element_type=jnp.float32
        )
        * score_scale
    )
    scores = jnp.where(keep, scores, -jnp.inf)
    peak = jnp.max(scores, axis=-1, keepdims=True)
    log_total = peak + jnp.log(jnp.sum(jnp.exp(scores - peak), axis=-1, keepdims=True))
    weights = jnp.exp(scores - log_total)
    rounded = weights.astype(jnp.bfloat16)
    output = jnp.einsum(
        "kgqt,tkd->qkgd", rounded, window_pair[1], preferred_element_type=jnp.float32
    )
    gate_open = jax.nn.sigmoid(gate_logits.astype(jnp.float32)).reshape(
        length, kv_heads, group, width
    )
    upstream = soft_cotangent.astype(jnp.float32).reshape(length, kv_heads, group, width)
    slope = (
        (upstream * output * gate_open * (1.0 - gate_open))
        .astype(jnp.bfloat16)
        .reshape(length, kv_heads * group, width)
    )
    gate_full = lax.dot_general(
        slope, gate_weight, (((1, 2), (1, 2)), ((), ())), preferred_element_type=jnp.float32
    )
    gate_part = gate_full.astype(jnp.bfloat16)
    gate_full, gate_part, inverse, queries, key_rows, value_rows = lax.optimization_barrier(
        (gate_full, gate_part, inverse, queries, key_rows, value_rows)
    )
    half = gate_part.shape[0] // 2
    head_index = lax.axis_index("head")
    kept = lax.dynamic_slice_in_dim(gate_full, head_index * half, half, 0)
    sent = lax.dynamic_slice_in_dim(gate_part, (1 - head_index) * half, half, 0)
    received = lax.ppermute(sent, "head", [(0, 1), (1, 0)])

    start_state = saved_state[0]
    cotangent = delta_cotangent.astype(jnp.float32)

    def forward_state(state_in):
        return delta_block(
            queries,
            key_rows,
            value_rows,
            write_strength,
            log_decay,
            state_in,
            segment,
            continued,
            inverse,
        )

    unused_state, state_pullback = jax.vjp(forward_state, start_state)
    own_part = state_pullback((cotangent, jnp.zeros_like(start_state)))[0]
    identity = jnp.broadcast_to(
        jnp.eye(start_state.shape[-1], dtype=jnp.float32), start_state.shape
    )
    transfer = delta_block(
        queries,
        key_rows,
        jnp.zeros_like(value_rows),
        write_strength,
        log_decay,
        identity,
        segment,
        continued,
        inverse,
    )[1]
    gathered = own_part
    incoming = own_part
    for step_index in range(HOPS):
        incoming = from_behind(shortened(gathered), "ctx", -1).astype(gathered.dtype)
        gathered = own_part + carry_back(incoming, transfer)

    received, incoming = lax.optimization_barrier((received, incoming))
    input_grad = kept + received.astype(jnp.float32)

    def forward(queries_in, keys_in, values_in, strength_in, decay_in):
        return delta_block(
            queries_in,
            keys_in,
            values_in,
            strength_in,
            decay_in,
            start_state,
            segment,
            continued,
            inverse,
        )

    unused, pullback = jax.vjp(forward, queries, key_rows, value_rows, write_strength, log_decay)
    readout_grad, address_grad, content_grad, strength_grad, decay_grad = pullback(
        (cotangent, incoming)
    )

    back = (upstream * gate_open).astype(jnp.bfloat16)
    row_dot = jnp.sum(back.astype(jnp.float32) * output, axis=-1).transpose(1, 2, 0)[..., None]
    dprob = jnp.einsum("qkgd,tkd->kgqt", back, window_pair[1], preferred_element_type=jnp.float32)
    dscore = (weights * (dprob - row_dot)).astype(jnp.bfloat16)
    query_grad = (
        jnp.einsum("kgqt,tkd->qkgd", dscore, window_pair[0], preferred_element_type=jnp.float32)
        * score_scale
    )
    query_grad = query_grad.reshape(length, kv_heads * group, width)
    key_part = (
        jnp.einsum("kgqt,qkgd->tkd", dscore, queries_four, preferred_element_type=jnp.float32)
        * score_scale
    )
    value_part = jnp.einsum("kgqt,qkgd->tkd", rounded, back, preferred_element_type=jnp.float32)
    returned = jnp.stack([key_part, value_part])

    def slab(distance):
        return returned[:, (HOPS - distance) * length : (HOPS - distance + 1) * length]

    summed = slab(0)
    for distance in range(1, HOPS + 1):
        summed = summed + from_behind(
            slab(distance).astype(jnp.bfloat16), "ctx", -distance
        ).astype(summed.dtype)
    return (
        readout_grad,
        address_grad,
        content_grad,
        strength_grad,
        decay_grad,
        query_grad,
        summed[0],
        summed[1],
        input_grad,
    )


def solution(mesh):
    placed = (
        P(),
        P("ctx", "head", None),
        P("ctx", "head", None),
        P("ctx", "head", None),
        P("ctx", "head"),
        P("ctx", "head"),
        P("ctx", "head", None, None),
        P("ctx", "head", None),
        P("ctx", "head", None),
        P("ctx", "head", None),
        P("ctx", "head", None),
        P("ctx", "head", None),
        P("ctx", "head", None),
        P(None, "head", None),
    )
    return jax.shard_map(
        shards,
        mesh=mesh,
        in_specs=placed,
        out_specs=(
            P("ctx", "head", None),
            P("ctx", "head", None),
            P("ctx", "head", None),
            P("ctx", "head"),
            P("ctx", "head"),
            P("ctx", "head", None),
            P("ctx", "head", None),
            P("ctx", "head", None),
            P(("ctx", "head"), None),
        ),
        check_vma=False,
    )
```
